1024 devices in a mesh: energy: 64 (over x, z), section: 16 (over y, core).
Axes of the slice: x: 4, y: 8, z: 16, core: 2. Of those that a mesh axis runs over, the one named last changes fastest.
Arguments:
- propagator: bfloat16 [64, 16, 2, 384, 384], P('energy', 'section')
- forward_source: bfloat16 [64, 16, 384, 128], P('energy', 'section'), may hold values from -6 to 6
- backward_source: bfloat16 [64, 16, 384, 128], P('energy', 'section'), may hold values from -6 to 6
- left_orbital: int32 [131072], P('section'), may hold values from 0 to 6143, as said below
- right_orbital: int32 [131072], P('section'), may hold values from 0 to 6143
- phonon_shift: int32 [8], replicated, may hold values from -6 to 6
- coupling: float32 [8, 131072], P(None, 'section'), may hold values from 0.1 to 1
Outputs:
- self_energy: float32 [2, 64, 131072], P(None, 'energy', 'section')
The draws below stay inside these ranges and needn't reach their ends.
Inputs may be any that keep to these rules, and one draw needn't show every extreme that they name: left_orbital[p] and right_orbital[p] are orbitals of section p // 8192: both lie from (p // 8192) * 384 to that plus 1 * 384 - 1, and they differ by at most 24.
All inputs are finite; a program needn't handle non-finite values.
Results may differ from the reference program's by a relative error of at most 0.022.
Values may be sent and summed in bfloat16 or wider, within the bound.
No kernel may reach another device: no remote copies, remote signals or barrier semaphores. Data moves between devices by JAX's collectives and lax.ppermute only.
A program may use at most 64 MiB of HBM per device.

```python
import math
import jax
import jax.numpy as jnp
from jax import lax

ORB = 384
RHS = 64
PHON = 8
SLAB_DEV = 1
NPAIR_DEV = 8192
ENERGIES = 64
SLABS = 16
NPAIRS = 131072
N_SECTION = 16


def draw_propagator(key, part):
    key_mag, key_angle, key_rand = jax.random.split(key, 3)
    diag_shape = (ENERGIES, SLABS, ORB)
    magnitude = jnp.exp(jax.random.uniform(key_mag, diag_shape, jnp.float32, math.log(0.55), math.log(0.9)))
    angle_draw = jax.random.uniform(key_angle, diag_shape, jnp.float32, -math.pi, math.pi)
    noise_scale = 0.18 / math.sqrt(2.0 * ORB)
    full_shape = (ENERGIES, SLABS, 2, ORB, ORB)
    random_part = jax.random.normal(key_rand, full_shape, jnp.float32) * noise_scale
    diagonal = jnp.stack([magnitude * jnp.cos(angle_draw), magnitude * jnp.sin(angle_draw)], axis=2)
    unit_matrix = jnp.eye(ORB, dtype=jnp.float32)
    return (random_part + diagonal[..., None] * unit_matrix).astype(jnp.bfloat16)


def pair_draw(key):
    inner = jax.random.fold_in(key, 7)
    key_left, key_step = jax.random.split(inner)
    span = SLAB_DEV * ORB
    position = jnp.arange(NPAIRS, dtype=jnp.int32)
    section = position // NPAIR_DEV
    within = position % NPAIR_DEV
    first = jax.random.randint(key_left, (NPAIRS,), 0, span, dtype=jnp.int32)
    offset_step = jax.random.randint(key_step, (NPAIRS,), -24, 25, dtype=jnp.int32)
    second = jnp.clip(first + offset_step, 0, span - 1)
    first = jnp.where(within == 0, 0, first)
    second = jnp.where(within == 0, 0, second)
    first = jnp.where(within == NPAIR_DEV - 1, span - 1, first)
    second = jnp.where(within == NPAIR_DEV - 1, span - 1, second)
    section_base = section * span
    return (first + section_base, second + section_base)


def draw_left_orbital(key, part):
    return pair_draw(key)[0]


def draw_right_orbital(key, part):
    return pair_draw(key)[1]


def with_ends(entries, key, least, high):
    longest = entries.shape.index(max(entries.shape))
    spots = []
    for shift in (0, 1):
        where = [jax.random.randint(jax.random.fold_in(key, axis), (), 0, length) for axis, length in enumerate(entries.shape)]
        where[longest] = (where[longest] + shift) % entries.shape[longest]
        spots.append(tuple(where))
    return entries.at[spots[0]].set(least).at[spots[1]].set(high)


def steps_of(own_key, dims, cuts, least, high):
    loudness, own = 1.0, jax.random.fold_in(own_key, 6)
    for axis_at, blocks in cuts:
        steps = jnp.exp(jax.random.uniform(jax.random.fold_in(own, axis_at), (blocks,), jnp.float32, least / len(cuts), high / len(cuts)))
        loudness = loudness * jnp.repeat(steps, dims[axis_at] // blocks).reshape([-1 if axis == axis_at else 1 for axis in range(len(dims))])
    return loudness


def centred(stream_key, extent, scale, reach, cuts=(), held_as=jnp.bfloat16):
    result = jax.random.normal(stream_key, extent, jnp.float32) * scale
    if len(cuts) > 0:
        result = steps_of(stream_key, extent, cuts, -0.22, 0.18) * result
    return jnp.clip(result, min=-reach, max=reach).astype(held_as)


def setup_inputs(seed: int = 0) -> dict:
    streams_of = jax.random.split(jax.random.key(seed), 8)
    return {
        "propagator": draw_propagator(jax.random.fold_in(streams_of[7], 71), 0),
        "forward_source": centred(streams_of[1], (ENERGIES, SLABS, ORB, 2 * RHS), 1.0, 6.0, ((0, 64), (1, 16))),
        "backward_source": centred(streams_of[2], (ENERGIES, SLABS, ORB, 2 * RHS), 1.0, 6.0, ((0, 64), (1, 16))),
        "left_orbital": draw_left_orbital(jax.random.fold_in(streams_of[7], 71), 0),
        "right_orbital": draw_right_orbital(jax.random.fold_in(streams_of[7], 71), 0),
        "phonon_shift": with_ends(jax.random.randint(streams_of[5], (PHON,), -6, 7), jax.random.fold_in(streams_of[5], 1), -6, 6).astype(jnp.int32),
        "coupling": jnp.clip(jnp.exp(math.log(1.0) - 2.3025851 * jax.random.uniform(streams_of[6], (PHON, NPAIRS), jnp.float32) ** steps_of(streams_of[6], (PHON, NPAIRS), ((1, 16),), -0.2, 0.2)), 0.1, 1.0),
    }


def complex_product(matrix, columns, adjoint):
    left_real = matrix.astype(jnp.float32)
    right_real = columns.astype(jnp.float32)
    half = right_real.shape[1] // 2
    if adjoint:
        product = jnp.einsum('cji,jn->cin', left_real, right_real, precision=lax.Precision.HIGHEST)
        real_part = product[0, :, :half] + product[1, :, half:]
        imag_part = product[0, :, half:] - product[1, :, :half]
    else:
        product = jnp.einsum('cij,jn->cin', left_real, right_real, precision=lax.Precision.HIGHEST)
        real_part = product[0, :, :half] - product[1, :, half:]
        imag_part = product[0, :, half:] + product[1, :, :half]
    return jnp.concatenate([real_part, imag_part], axis=1)


def as_pair(joined):
    width = joined.shape[0]
    return jnp.stack([joined[:, :width], joined[:, width:]])


def section_maps(blocks, forward_src, backward_src):
    count = blocks.shape[0]
    composite = jnp.concatenate([blocks[0, 0], blocks[0, 1]], axis=1)
    forward_part = forward_src[0]
    for j in range(1, count):
        composite = complex_product(blocks[j], composite, False).astype(jnp.bfloat16)
        forward_part = (complex_product(blocks[j], forward_part, False) + forward_src[j]).astype(jnp.bfloat16)
    backward_part = backward_src[count - 1]
    for j in range(count - 2, -1, -1):
        backward_part = (complex_product(blocks[j], backward_part, True) + backward_src[j]).astype(jnp.bfloat16)
    return composite, forward_part, backward_part


def forward_pass(blocks, sources, start_state):
    current = start_state
    results = []
    for j in range(blocks.shape[0]):
        current = (complex_product(blocks[j], current, False) + sources[j]).astype(jnp.bfloat16)
        results.append(current)
    return jnp.stack(results)


def backward_pass(blocks, sources, start_state):
    current = start_state
    results = [None] * blocks.shape[0]
    for j in range(blocks.shape[0] - 1, -1, -1):
        current = (complex_product(blocks[j], current, True) + sources[j]).astype(jnp.bfloat16)
        results[j] = current
    return jnp.stack(results)


def lesser(field_rows, adjoint_rows, left_index, right_index, modes):
    left_rows = jnp.take(field_rows, left_index, axis=0).astype(jnp.float32)
    right_rows = jnp.take(adjoint_rows, right_index, axis=0).astype(jnp.float32)
    real_part = jnp.sum(left_rows[:, :modes] * right_rows[:, :modes] + left_rows[:, modes:] * right_rows[:, modes:], axis=1)
    imag_part = jnp.sum(left_rows[:, modes:] * right_rows[:, :modes] - left_rows[:, :modes] * right_rows[:, modes:], axis=1)
    return jnp.stack([real_part, imag_part]) * (modes ** -0.5)


def shifted_sum(portion, begin_at, own_energy, phonon_shift, coupling):
    count = portion.shape[1]
    positions = begin_at + jnp.arange(count, dtype=jnp.int32)
    summed = jnp.zeros((portion.shape[0], own_energy.shape[0], portion.shape[2]), jnp.float32)
    for k in range(phonon_shift.shape[0]):
        selector = (positions[None, :] == (own_energy - phonon_shift[k])[:, None]).astype(jnp.float32)
        moved = jnp.einsum('ef,cfp->cep', selector, portion.astype(jnp.float32), precision=lax.Precision.HIGHEST)
        summed = summed + coupling[k][None, None, :] * moved
    return summed


def reference(propagator, forward_source, backward_source, left_orbital, right_orbital, phonon_shift, coupling):
    def per_energy(members):
        blocks_all, forward_all, backward_all = members
        blocks = blocks_all.reshape(N_SECTION, SLAB_DEV, 2, ORB, ORB)
        forward_src = forward_all.reshape(N_SECTION, SLAB_DEV, ORB, 2 * RHS)
        backward_src = backward_all.reshape(N_SECTION, SLAB_DEV, ORB, 2 * RHS)
        composite, forward_part, backward_part = jax.vmap(section_maps)(blocks, forward_src, backward_src)
        zero_state = jnp.zeros((ORB, 2 * RHS), jnp.bfloat16)

        def forward_step(current, parts):
            matrix, vector = parts
            following = (complex_product(as_pair(matrix), current, False) + vector).astype(jnp.bfloat16)
            return following, current

        def backward_step(current, parts):
            matrix, vector = parts
            following = (complex_product(as_pair(matrix), current, True) + vector).astype(jnp.bfloat16)
            return following, current

        final_fwd, incoming = lax.scan(forward_step, zero_state, (composite, forward_part))
        final_bwd, returning = lax.scan(backward_step, zero_state, (composite, backward_part), reverse=True)
        fields = jax.vmap(forward_pass)(blocks, forward_src, incoming)
        adjoints = jax.vmap(backward_pass)(blocks, backward_src, returning)
        return lesser(fields.reshape(-1, 2 * RHS), adjoints.reshape(-1, 2 * RHS), left_orbital, right_orbital, RHS)

    lesser_part = lax.map(per_energy, (propagator, forward_source, backward_source))
    lesser_part = jnp.transpose(lesser_part, (1, 0, 2))
    return shifted_sum(lesser_part, jnp.int32(0), jnp.arange(ENERGIES, dtype=jnp.int32), phonon_shift, coupling)
```

```python
import jax
import jax.numpy as jnp
from jax import lax
from jax.sharding import PartitionSpec as P

MAX_SHIFT = 6


def passed_along(value, axis, steps):
    count = lax.axis_size(axis)
    leading, last = (max(0, -steps), min(count, count - steps))
    return lax.ppermute(value, axis, [(source, source + steps) for source in range(leading, last)])


def complex_product(matrix, columns, adjoint):
    half = columns.shape[1] // 2
    if adjoint:
        product = jnp.einsum("cji,jn->cin", matrix, columns, preferred_element_type=jnp.float32)
        real_part = product[0, :, :half] + product[1, :, half:]
        imag_part = product[0, :, half:] - product[1, :, :half]
    else:
        product = jnp.einsum("cij,jn->cin", matrix, columns, preferred_element_type=jnp.float32)
        real_part = product[0, :, :half] - product[1, :, half:]
        imag_part = product[0, :, half:] + product[1, :, :half]
    return jnp.concatenate([real_part, imag_part], axis=1)


def picked_rows(table, index):
    rows = table.shape[0]
    selector = (lax.broadcasted_iota(jnp.int32, (rows, index.shape[0]), 0) == index[None, :])
    return jnp.einsum(
        "ar,ap->rp", table, selector.astype(table.dtype), preferred_element_type=jnp.float32
    )


def on_device(
    propagator, forward_source, backward_source, left_orbital, right_orbital, phonon_shift, coupling
):
    orbitals = propagator.shape[3]
    modes = forward_source.shape[3] // 2
    blocks = propagator[0, 0]
    forward_src = forward_source[0, 0]
    backward_src = backward_source[0, 0]
    relay_turns = lax.axis_size("section") - 1

    def relay_turn(turn_index, state):
        fields, adjoints = state
        incoming = passed_along(fields, "section", 1)
        returning = passed_along(adjoints, "section", -1)
        fields = (complex_product(blocks, incoming, False) + forward_src).astype(jnp.bfloat16)
        adjoints = (complex_product(blocks, returning, True) + backward_src).astype(jnp.bfloat16)
        return fields, adjoints

    fields, adjoints = lax.fori_loop(0, relay_turns, relay_turn, (forward_src, backward_src))

    section_base = lax.axis_index("section") * orbitals
    left_rows = picked_rows(fields, left_orbital - section_base)
    right_rows = picked_rows(adjoints, right_orbital - section_base)
    real_part = jnp.sum(left_rows * right_rows, axis=0)
    imag_part = jnp.sum(left_rows[modes:] * right_rows[:modes], axis=0) - jnp.sum(
        left_rows[:modes] * right_rows[modes:], axis=0
    )
    lesser_part = jnp.stack([real_part, imag_part]) * modes ** (-0.5)

    sent = lesser_part.astype(jnp.bfloat16)
    self_energy = jnp.zeros_like(lesser_part)
    for offset in range(-MAX_SHIFT, MAX_SHIFT + 1):
        weight = jnp.sum(jnp.where((phonon_shift == offset)[:, None], coupling, 0.0), axis=0)
        if offset == 0:
            moved = lesser_part
        else:
            moved = passed_along(sent, "energy", offset).astype(jnp.float32)
        self_energy = self_energy + weight[None, :] * moved
    return self_energy[:, None, :]


def solution(mesh):
    placed = (
        P("energy", "section", None, None, None),
        P("energy", "section", None, None),
        P("energy", "section", None, None),
        P("section"),
        P("section"),
        P(),
        P(None, "section"),
    )
    return jax.shard_map(
        on_device,
        mesh=mesh,
        in_specs=placed,
        out_specs=P(None, "energy", "section"),
        check_vma=False,
    )
```

```python
import jax
import jax.numpy as jnp
from jax import lax
from jax.sharding import PartitionSpec as P

MAX_SHIFT = 6


def passed_along(value, axis, steps):
    count = lax.axis_size(axis)
    leading, last = (max(0, -steps), min(count, count - steps))
    return lax.ppermute(value, axis, [(source, source + steps) for source in range(leading, last)])


def complex_product(matrix, columns, adjoint):
    half = columns.shape[1] // 2
    if adjoint:
        product = jnp.einsum("cji,jn->cin", matrix, columns, preferred_element_type=jnp.float32)
        real_part = product[0, :, :half] + product[1, :, half:]
        imag_part = product[0, :, half:] - product[1, :, :half]
    else:
        product = jnp.einsum("cij,jn->cin", matrix, columns, preferred_element_type=jnp.float32)
        real_part = product[0, :, :half] - product[1, :, half:]
        imag_part = product[0, :, half:] + product[1, :, :half]
    return jnp.concatenate([real_part, imag_part], axis=1)


def matrix_product(left, right):
    product = jnp.einsum("cij,djk->cdik", left, right, preferred_element_type=jnp.float32)
    real_part = product[0, 0] - product[1, 1]
    imag_part = product[0, 1] + product[1, 0]
    return jnp.stack([real_part, imag_part]).astype(jnp.bfloat16)


def picked_rows(table, index):
    rows = table.shape[0]
    selector = (lax.broadcasted_iota(jnp.int32, (rows, index.shape[0]), 0) == index[None, :])
    return jnp.einsum(
        "ar,ap->rp", table, selector.astype(table.dtype), preferred_element_type=jnp.float32
    )


def sweeps(blocks, forward_src, backward_src):
    count = lax.axis_size("section")
    odd = lax.axis_index("section") % 2 == 1
    swap = [(2 * y + side, 2 * y + 1 - side) for y in range(count // 2) for side in (0, 1)]
    other_blocks, other_src = lax.ppermute(
        (blocks, jnp.where(odd, backward_src, forward_src)), "section", swap
    )
    pair_map = matrix_product(
        jnp.where(odd, blocks, other_blocks), jnp.where(odd, other_blocks, blocks)
    )
    pair_forward = (complex_product(blocks, other_src, False) + forward_src).astype(jnp.bfloat16)
    pair_backward = (complex_product(blocks, other_src, True) + backward_src).astype(jnp.bfloat16)
    pair_adjoint = jnp.stack([pair_map[0].T, -pair_map[1].T])
    chain_map = jnp.where(odd, pair_map, pair_adjoint)
    chain_src = jnp.where(odd, pair_forward, pair_backward)
    chain = [(2 * y + 1, 2 * y + 3) for y in range(count // 2 - 1)]
    chain += [(2 * y, 2 * y - 2) for y in range(1, count // 2)]
    state = chain_src
    for _ in range(count // 2 - 1):
        state = (complex_product(chain_map, lax.ppermute(state, "section", chain), False)
                 + chain_src).astype(jnp.bfloat16)
    hand_over = [(s, s + 1) for s in range(1, count - 1, 2)]
    hand_over += [(s, s - 1) for s in range(2, count, 2)]
    neighbour = lax.ppermute(state, "section", hand_over)
    fields = jnp.where(
        odd, state, (complex_product(blocks, neighbour, False) + forward_src).astype(jnp.bfloat16)
    )
    adjoints = jnp.where(
        odd, (complex_product(blocks, neighbour, True) + backward_src).astype(jnp.bfloat16), state
    )
    return fields, adjoints


def shifted_copies(sent, direction):
    copies = []
    step = 1
    while len(copies) < MAX_SHIFT:
        width = min(step, MAX_SHIFT - len(copies))
        payload = jnp.stack(([sent] + copies)[:width])
        arrived = passed_along(payload, "energy", direction * step)
        copies.extend(arrived[j] for j in range(width))
        step *= 2
    return copies


def on_device(
    propagator, forward_source, backward_source, left_orbital, right_orbital, phonon_shift, coupling
):
    orbitals = propagator.shape[3]
    modes = forward_source.shape[3] // 2
    fields, adjoints = sweeps(propagator[0, 0], forward_source[0, 0], backward_source[0, 0])

    section_base = lax.axis_index("section") * orbitals
    left_rows = picked_rows(fields, left_orbital - section_base)
    right_rows = picked_rows(adjoints, right_orbital - section_base)
    real_part = jnp.sum(left_rows * right_rows, axis=0)
    imag_part = jnp.sum(left_rows[modes:] * right_rows[:modes], axis=0) - jnp.sum(
        left_rows[:modes] * right_rows[modes:], axis=0
    )
    lesser_part = jnp.stack([real_part, imag_part]) * modes ** (-0.5)

    sent = lesser_part.astype(jnp.bfloat16)
    moved = {0: lesser_part}
    for direction in (1, -1):
        for j, copy in enumerate(shifted_copies(sent, direction)):
            moved[direction * (j + 1)] = copy.astype(jnp.float32)
    self_energy = jnp.zeros_like(lesser_part)
    for offset in range(-MAX_SHIFT, MAX_SHIFT + 1):
        weight = jnp.sum(jnp.where((phonon_shift == offset)[:, None], coupling, 0.0), axis=0)
        self_energy = self_energy + weight[None, :] * moved[offset]
    return self_energy[:, None, :]


def solution(mesh):
    placed = (
        P("energy", "section", None, None, None),
        P("energy", "section", None, None),
        P("energy", "section", None, None),
        P("section"),
        P("section"),
        P(),
        P(None, "section"),
    )
    return jax.shard_map(
        on_device,
        mesh=mesh,
        in_specs=placed,
        out_specs=P(None, "energy", "section"),
        check_vma=False,
    )
```

```python
import jax
import jax.numpy as jnp
from jax import lax
from jax.sharding import PartitionSpec as P

MAX_SHIFT = 6


def passed_along(value, axis, steps):
    count = lax.axis_size(axis)
    leading, last = (max(0, -steps), min(count, count - steps))
    return lax.ppermute(value, axis, [(source, source + steps) for source in range(leading, last)])


def complex_product(matrix, columns, adjoint):
    half = columns.shape[1] // 2
    if adjoint:
        product = jnp.einsum("cji,jn->cin", matrix, columns, preferred_element_type=jnp.float32)
        real_part = product[0, :, :half] + product[1, :, half:]
        imag_part = product[0, :, half:] - product[1, :, :half]
    else:
        product = jnp.einsum("cij,jn->cin", matrix, columns, preferred_element_type=jnp.float32)
        real_part = product[0, :, :half] - product[1, :, half:]
        imag_part = product[0, :, half:] + product[1, :, :half]
    return jnp.concatenate([real_part, imag_part], axis=1)


def matrix_product(left, right):
    product = jnp.einsum("cij,djk->cdik", left, right, preferred_element_type=jnp.float32)
    real_part = product[0, 0] - product[1, 1]
    imag_part = product[0, 1] + product[1, 0]
    return real_part, imag_part


def adjoint_product(left, right):
    product = jnp.einsum("ckj,dji->cdik", left, right, preferred_element_type=jnp.float32)
    real_part = product[0, 0] - product[1, 1]
    imag_part = -(product[0, 1] + product[1, 0])
    return real_part, imag_part


def stacked(columns):
    half = columns.shape[1] // 2
    return jnp.concatenate([columns[:, :half], columns[:, half:]], axis=0)


def joined(rows):
    half = rows.shape[0] // 2
    return jnp.concatenate([rows[:half], rows[half:]], axis=1)


def picked_rows(table, index):
    rows = table.shape[0]
    selector = (lax.broadcasted_iota(jnp.int32, (rows, index.shape[0]), 0) == index[None, :])
    return jnp.einsum(
        "ar,ap->rp", table, selector.astype(table.dtype), preferred_element_type=jnp.float32
    )


def sweeps(blocks, forward_src, backward_src):
    count = lax.axis_size("section")
    odd = lax.axis_index("section") % 2 == 1
    swap = [(2 * y + side, 2 * y + 1 - side) for y in range(count // 2) for side in (0, 1)]
    other_blocks, other_src = lax.ppermute(
        (blocks, jnp.where(odd, backward_src, forward_src)), "section", swap
    )
    left = jnp.where(odd, blocks, other_blocks)
    right = jnp.where(odd, other_blocks, blocks)
    forward_real, forward_imag = matrix_product(left, right)
    backward_real, backward_imag = adjoint_product(left, right)
    real_part = jnp.where(odd, forward_real, backward_real).astype(jnp.bfloat16)
    imag_part = jnp.where(odd, forward_imag, backward_imag).astype(jnp.bfloat16)
    chain_map = jnp.concatenate(
        [
            jnp.concatenate([real_part, -imag_part], axis=1),
            jnp.concatenate([imag_part, real_part], axis=1),
        ],
        axis=0,
    )
    pair_forward = (complex_product(blocks, other_src, False) + forward_src).astype(jnp.bfloat16)
    pair_backward = (complex_product(blocks, other_src, True) + backward_src).astype(jnp.bfloat16)
    chain_src = stacked(jnp.where(odd, pair_forward, pair_backward))
    chain = [(2 * y + 1, 2 * y + 3) for y in range(count // 2 - 1)]
    chain += [(2 * y, 2 * y - 2) for y in range(1, count // 2)]
    state = chain_src
    for _ in range(count // 2 - 1):
        arrived = lax.ppermute(state, "section", chain)
        state = (jnp.dot(chain_map, arrived, preferred_element_type=jnp.float32)
                 + chain_src).astype(jnp.bfloat16)
    state = joined(state)
    hand_over = [(s, s + 1) for s in range(1, count - 1, 2)]
    hand_over += [(s, s - 1) for s in range(2, count, 2)]
    neighbour = lax.ppermute(state, "section", hand_over)
    fields = jnp.where(
        odd, state, (complex_product(blocks, neighbour, False) + forward_src).astype(jnp.bfloat16)
    )
    adjoints = jnp.where(
        odd, (complex_product(blocks, neighbour, True) + backward_src).astype(jnp.bfloat16), state
    )
    return fields, adjoints


def shifted_copies(sent, direction):
    copies = []
    step = 1
    while len(copies) < MAX_SHIFT:
        width = min(step, MAX_SHIFT - len(copies))
        payload = jnp.stack(([sent] + copies)[:width])
        arrived = passed_along(payload, "energy", direction * step)
        copies.extend(arrived[j] for j in range(width))
        step *= 2
    return copies


def on_device(
    propagator, forward_source, backward_source, left_orbital, right_orbital, phonon_shift, coupling
):
    orbitals = propagator.shape[3]
    modes = forward_source.shape[3] // 2
    fields, adjoints = sweeps(propagator[0, 0], forward_source[0, 0], backward_source[0, 0])

    section_base = lax.axis_index("section") * orbitals
    left_rows = picked_rows(fields, left_orbital - section_base)
    right_rows = picked_rows(adjoints, right_orbital - section_base)
    real_part = jnp.sum(left_rows * right_rows, axis=0)
    imag_part = jnp.sum(left_rows[modes:] * right_rows[:modes], axis=0) - jnp.sum(
        left_rows[:modes] * right_rows[modes:], axis=0
    )
    lesser_part = jnp.stack([real_part, imag_part]) * modes ** (-0.5)

    sent = lesser_part.astype(jnp.bfloat16)
    moved = {0: lesser_part}
    for direction in (1, -1):
        for j, copy in enumerate(shifted_copies(sent, direction)):
            moved[direction * (j + 1)] = copy.astype(jnp.float32)
    self_energy = jnp.zeros_like(lesser_part)
    for offset in range(-MAX_SHIFT, MAX_SHIFT + 1):
        weight = jnp.sum(jnp.where((phonon_shift == offset)[:, None], coupling, 0.0), axis=0)
        self_energy = self_energy + weight[None, :] * moved[offset]
    return self_energy[:, None, :]


def solution(mesh):
    placed = (
        P("energy", "section", None, None, None),
        P("energy", "section", None, None),
        P("energy", "section", None, None),
        P("section"),
        P("section"),
        P(),
        P(None, "section"),
    )
    return jax.shard_map(
        on_device,
        mesh=mesh,
        in_specs=placed,
        out_specs=P(None, "energy", "section"),
        check_vma=False,
    )
```

```python
import jax
import jax.numpy as jnp
from jax import lax
from jax.sharding import PartitionSpec as P

MAX_SHIFT = 6


def passed_along(value, axis, steps):
    count = lax.axis_size(axis)
    leading, last = (max(0, -steps), min(count, count - steps))
    return lax.ppermute(value, axis, [(source, source + steps) for source in range(leading, last)])


def complex_product(matrix, columns, adjoint):
    half = columns.shape[1] // 2
    if adjoint:
        product = jnp.einsum("cji,jn->cin", matrix, columns, preferred_element_type=jnp.float32)
        real_part = product[0, :, :half] + product[1, :, half:]
        imag_part = product[0, :, half:] - product[1, :, :half]
    else:
        product = jnp.einsum("cij,jn->cin", matrix, columns, preferred_element_type=jnp.float32)
        real_part = product[0, :, :half] - product[1, :, half:]
        imag_part = product[0, :, half:] + product[1, :, :half]
    return jnp.concatenate([real_part, imag_part], axis=1)


def matrix_product(left, right):
    product = jnp.einsum("cij,djk->cdik", left, right, preferred_element_type=jnp.float32)
    real_part = product[0, 0] - product[1, 1]
    imag_part = product[0, 1] + product[1, 0]
    return real_part, imag_part


def adjoint_product(left, right):
    product = jnp.einsum("ckj,dji->cdik", left, right, preferred_element_type=jnp.float32)
    real_part = product[0, 0] - product[1, 1]
    imag_part = -(product[0, 1] + product[1, 0])
    return real_part, imag_part


def stacked(columns):
    half = columns.shape[1] // 2
    return jnp.concatenate([columns[:, :half], columns[:, half:]], axis=0)


def joined(rows):
    half = rows.shape[0] // 2
    return jnp.concatenate([rows[:half], rows[half:]], axis=1)


def picked_rows(table, index):
    rows = table.shape[0]
    selector = (lax.broadcasted_iota(jnp.int32, (rows, index.shape[0]), 0) == index[None, :])
    return jnp.einsum(
        "ar,ap->rp", table, selector.astype(table.dtype), preferred_element_type=jnp.float32
    )


def sweeps(blocks, forward_src, backward_src):
    count = lax.axis_size("section")
    odd = lax.axis_index("section") % 2 == 1
    swap = [(2 * y + side, 2 * y + 1 - side) for y in range(count // 2) for side in (0, 1)]
    other_blocks, other_src = lax.ppermute(
        (blocks, jnp.where(odd, backward_src, forward_src)), "section", swap
    )
    left = jnp.where(odd, blocks, other_blocks)
    right = jnp.where(odd, other_blocks, blocks)
    forward_real, forward_imag = matrix_product(left, right)
    backward_real, backward_imag = adjoint_product(left, right)
    real_part = jnp.where(odd, forward_real, backward_real).astype(jnp.bfloat16)
    imag_part = jnp.where(odd, forward_imag, backward_imag).astype(jnp.bfloat16)
    chain_map = jnp.concatenate(
        [
            jnp.concatenate([real_part, -imag_part], axis=1),
            jnp.concatenate([imag_part, real_part], axis=1),
        ],
        axis=0,
    )
    pair_forward = (complex_product(blocks, other_src, False) + forward_src).astype(jnp.bfloat16)
    pair_backward = (complex_product(blocks, other_src, True) + backward_src).astype(jnp.bfloat16)
    chain_src = stacked(jnp.where(odd, pair_forward, pair_backward))
    chips = count // 2
    chip = lax.axis_index("section") // 2
    chain = [(2 * y + 1, 2 * y + 3) for y in range(chips - 1)]
    chain += [(2 * y, 2 * y - 2) for y in range(1, chips)]
    own_map = jnp.stack([real_part, imag_part])
    upstream_map, upstream_src = lax.ppermute((own_map, chain_src), "section", chain)
    has_upstream = jnp.where(odd, chip >= 1, chip <= chips - 2)
    joint_real, joint_imag = matrix_product(own_map, upstream_map)
    joint_real = jnp.where(has_upstream, joint_real, real_part).astype(jnp.bfloat16)
    joint_imag = jnp.where(has_upstream, joint_imag, imag_part).astype(jnp.bfloat16)
    joint_src = (jnp.dot(chain_map, upstream_src, preferred_element_type=jnp.float32)
                 + chain_src).astype(jnp.bfloat16)
    joint_map = jnp.concatenate(
        [
            jnp.concatenate([joint_real, -joint_imag], axis=1),
            jnp.concatenate([joint_imag, joint_real], axis=1),
        ],
        axis=0,
    )
    stride = [(2 * y + 1, 2 * y + 5) for y in range(chips - 2)]
    stride += [(2 * y, 2 * y - 4) for y in range(2, chips)]
    state = joint_src
    for _ in range((chips - 1) // 2):
        arrived = lax.ppermute(state, "section", stride)
        state = (jnp.dot(joint_map, arrived, preferred_element_type=jnp.float32)
                 + joint_src).astype(jnp.bfloat16)
    state = joined(state)
    hand_over = [(s, s + 1) for s in range(1, count - 1, 2)]
    hand_over += [(s, s - 1) for s in range(2, count, 2)]
    neighbour = lax.ppermute(state, "section", hand_over)
    fields = jnp.where(
        odd, state, (complex_product(blocks, neighbour, False) + forward_src).astype(jnp.bfloat16)
    )
    adjoints = jnp.where(
        odd, (complex_product(blocks, neighbour, True) + backward_src).astype(jnp.bfloat16), state
    )
    return fields, adjoints


def shifted_copies(sent, direction):
    copies = []
    step = 1
    while len(copies) < MAX_SHIFT:
        width = min(step, MAX_SHIFT - len(copies))
        payload = jnp.stack(([sent] + copies)[:width])
        arrived = passed_along(payload, "energy", direction * step)
        copies.extend(arrived[j] for j in range(width))
        step *= 2
    return copies


def on_device(
    propagator, forward_source, backward_source, left_orbital, right_orbital, phonon_shift, coupling
):
    orbitals = propagator.shape[3]
    modes = forward_source.shape[3] // 2
    fields, adjoints = sweeps(propagator[0, 0], forward_source[0, 0], backward_source[0, 0])

    section_base = lax.axis_index("section") * orbitals
    left_rows = picked_rows(fields, left_orbital - section_base)
    right_rows = picked_rows(adjoints, right_orbital - section_base)
    real_part = jnp.sum(left_rows * right_rows, axis=0)
    imag_part = jnp.sum(left_rows[modes:] * right_rows[:modes], axis=0) - jnp.sum(
        left_rows[:modes] * right_rows[modes:], axis=0
    )
    lesser_part = jnp.stack([real_part, imag_part]) * modes ** (-0.5)

    sent = lesser_part.astype(jnp.bfloat16)
    moved = {0: lesser_part}
    for direction in (1, -1):
        for j, copy in enumerate(shifted_copies(sent, direction)):
            moved[direction * (j + 1)] = copy.astype(jnp.float32)
    self_energy = jnp.zeros_like(lesser_part)
    for offset in range(-MAX_SHIFT, MAX_SHIFT + 1):
        weight = jnp.sum(jnp.where((phonon_shift == offset)[:, None], coupling, 0.0), axis=0)
        self_energy = self_energy + weight[None, :] * moved[offset]
    return self_energy[:, None, :]


def solution(mesh):
    placed = (
        P("energy", "section", None, None, None),
        P("energy", "section", None, None),
        P("energy", "section", None, None),
        P("section"),
        P("section"),
        P(),
        P(None, "section"),
    )
    return jax.shard_map(
        on_device,
        mesh=mesh,
        in_specs=placed,
        out_specs=P(None, "energy", "section"),
        check_vma=False,
    )
```

```python
import jax
import jax.numpy as jnp
from jax import lax
from jax.sharding import PartitionSpec as P

MAX_SHIFT = 6


def passed_along(value, axis, steps):
    count = lax.axis_size(axis)
    leading, last = (max(0, -steps), min(count, count - steps))
    return lax.ppermute(value, axis, [(source, source + steps) for source in range(leading, last)])


def complex_product(matrix, columns, adjoint):
    half = columns.shape[1] // 2
    if adjoint:
        product = jnp.einsum("cji,jn->cin", matrix, columns, preferred_element_type=jnp.float32)
        real_part = product[0, :, :half] + product[1, :, half:]
        imag_part = product[0, :, half:] - product[1, :, :half]
    else:
        product = jnp.einsum("cij,jn->cin", matrix, columns, preferred_element_type=jnp.float32)
        real_part = product[0, :, :half] - product[1, :, half:]
        imag_part = product[0, :, half:] + product[1, :, :half]
    return jnp.concatenate([real_part, imag_part], axis=1)


def matrix_product(left, right):
    product = jnp.einsum("cij,djk->cdik", left, right, preferred_element_type=jnp.float32)
    real_part = product[0, 0] - product[1, 1]
    imag_part = product[0, 1] + product[1, 0]
    return real_part, imag_part


def adjoint_product(left, right):
    product = jnp.einsum("ckj,dji->cdik", left, right, preferred_element_type=jnp.float32)
    real_part = product[0, 0] - product[1, 1]
    imag_part = -(product[0, 1] + product[1, 0])
    return real_part, imag_part


def stacked(columns):
    half = columns.shape[1] // 2
    return jnp.concatenate([columns[:, :half], columns[:, half:]], axis=0)


def joined(rows):
    half = rows.shape[0] // 2
    return jnp.concatenate([rows[:half], rows[half:]], axis=1)


def picked_rows(table, index):
    rows = table.shape[0]
    selector = (lax.broadcasted_iota(jnp.int32, (rows, index.shape[0]), 0) == index[None, :])
    return jnp.einsum(
        "ar,ap->rp", table, selector.astype(table.dtype), preferred_element_type=jnp.float32
    )


def sweeps(blocks, forward_src, backward_src):
    count = lax.axis_size("section")
    odd = lax.axis_index("section") % 2 == 1
    swap = [(2 * y + side, 2 * y + 1 - side) for y in range(count // 2) for side in (0, 1)]
    other_blocks, other_src = lax.ppermute(
        (blocks, jnp.where(odd, backward_src, forward_src)), "section", swap
    )
    left = jnp.where(odd, blocks, other_blocks)
    right = jnp.where(odd, other_blocks, blocks)
    forward_real, forward_imag = matrix_product(left, right)
    backward_real, backward_imag = adjoint_product(left, right)
    real_part = jnp.where(odd, forward_real, backward_real).astype(jnp.bfloat16)
    imag_part = jnp.where(odd, forward_imag, backward_imag).astype(jnp.bfloat16)
    chain_map = jnp.concatenate(
        [
            jnp.concatenate([real_part, -imag_part], axis=1),
            jnp.concatenate([imag_part, real_part], axis=1),
        ],
        axis=0,
    )
    pair_forward = (complex_product(blocks, other_src, False) + forward_src).astype(jnp.bfloat16)
    pair_backward = (complex_product(blocks, other_src, True) + backward_src).astype(jnp.bfloat16)
    chain_src = stacked(jnp.where(odd, pair_forward, pair_backward))
    chips = count // 2
    chip = lax.axis_index("section") // 2
    chain = [(2 * y + 1, 2 * y + 3) for y in range(chips - 1)]
    chain += [(2 * y, 2 * y - 2) for y in range(1, chips)]
    own_map = jnp.stack([real_part, imag_part])
    upstream_map, upstream_src = lax.ppermute((own_map, chain_src), "section", chain)
    has_upstream = jnp.where(odd, chip >= 1, chip <= chips - 2)
    joint_real, joint_imag = matrix_product(own_map, upstream_map)
    joint_real = jnp.where(has_upstream, joint_real, real_part).astype(jnp.bfloat16)
    joint_imag = jnp.where(has_upstream, joint_imag, imag_part).astype(jnp.bfloat16)
    joint_src = (jnp.dot(chain_map, upstream_src, preferred_element_type=jnp.float32)
                 + chain_src).astype(jnp.bfloat16)
    joint_map = jnp.concatenate(
        [
            jnp.concatenate([joint_real, -joint_imag], axis=1),
            jnp.concatenate([joint_imag, joint_real], axis=1),
        ],
        axis=0,
    )
    stride = [(2 * y + 1, 2 * y + 5) for y in range(chips - 2)]
    stride += [(2 * y, 2 * y - 4) for y in range(2, chips)]
    state = joint_src
    for _ in range((chips - 1) // 2):
        arrived = lax.ppermute(state, "section", stride)
        state = (jnp.dot(joint_map, arrived, preferred_element_type=jnp.float32)
                 + joint_src).astype(jnp.bfloat16)
    state = joined(state)
    hand_over = [(s, s + 1) for s in range(1, count - 1, 2)]
    hand_over += [(s, s - 1) for s in range(2, count, 2)]
    neighbour = lax.ppermute(state, "section", hand_over)
    fields = jnp.where(
        odd, state, (complex_product(blocks, neighbour, False) + forward_src).astype(jnp.bfloat16)
    )
    adjoints = jnp.where(
        odd, (complex_product(blocks, neighbour, True) + backward_src).astype(jnp.bfloat16), state
    )
    return fields, adjoints


def shifted_copies(sent, direction):
    copies = []
    step = 1
    while len(copies) < MAX_SHIFT:
        width = min(step, MAX_SHIFT - len(copies))
        payload = jnp.stack(([sent] + copies)[:width])
        arrived = passed_along(payload, "energy", direction * step)
        copies.extend(arrived[j] for j in range(width))
        step *= 2
    return copies


def on_device(
    propagator, forward_source, backward_source, left_orbital, right_orbital, phonon_shift, coupling
):
    orbitals = propagator.shape[3]
    modes = forward_source.shape[3] // 2
    fields, adjoints = sweeps(propagator[0, 0], forward_source[0, 0], backward_source[0, 0])

    section_base = lax.axis_index("section") * orbitals
    left_rows = picked_rows(fields, left_orbital - section_base)
    right_rows = picked_rows(adjoints, right_orbital - section_base)
    real_part = jnp.sum(left_rows * right_rows, axis=0)
    imag_part = jnp.sum(left_rows[modes:] * right_rows[:modes], axis=0) - jnp.sum(
        left_rows[:modes] * right_rows[modes:], axis=0
    )
    lesser_part = jnp.stack([real_part, imag_part]) * modes ** (-0.5)

    sent = lesser_part.astype(jnp.bfloat16)
    gathered = lax.all_gather(sent, "energy")
    energy = lax.axis_index("energy")
    last = gathered.shape[0] - 1
    moved = {0: lesser_part}
    for offset in range(-MAX_SHIFT, MAX_SHIFT + 1):
        if offset != 0:
            source = energy - offset
            picked = lax.dynamic_index_in_dim(gathered, jnp.clip(source, 0, last), 0, False)
            inside = (source >= 0) & (source <= last)
            moved[offset] = jnp.where(inside, picked.astype(jnp.float32), 0.0)
    self_energy = jnp.zeros_like(lesser_part)
    for offset in range(-MAX_SHIFT, MAX_SHIFT + 1):
        weight = jnp.sum(jnp.where((phonon_shift == offset)[:, None], coupling, 0.0), axis=0)
        self_energy = self_energy + weight[None, :] * moved[offset]
    return self_energy[:, None, :]


def solution(mesh):
    placed = (
        P("energy", "section", None, None, None),
        P("energy", "section", None, None),
        P("energy", "section", None, None),
        P("section"),
        P("section"),
        P(),
        P(None, "section"),
    )
    return jax.shard_map(
        on_device,
        mesh=mesh,
        in_specs=placed,
        out_specs=P(None, "energy", "section"),
        check_vma=False,
    )
```

```python
import jax
import jax.numpy as jnp
from jax import lax
from jax.sharding import PartitionSpec as P

MAX_SHIFT = 6


def passed_along(value, axis, steps):
    count = lax.axis_size(axis)
    leading, last = (max(0, -steps), min(count, count - steps))
    return lax.ppermute(value, axis, [(source, source + steps) for source in range(leading, last)])


def complex_product(matrix, columns, adjoint):
    half = columns.shape[1] // 2
    if adjoint:
        product = jnp.einsum("cji,jn->cin", matrix, columns, preferred_element_type=jnp.float32)
        real_part = product[0, :, :half] + product[1, :, half:]
        imag_part = product[0, :, half:] - product[1, :, :half]
    else:
        product = jnp.einsum("cij,jn->cin", matrix, columns, preferred_element_type=jnp.float32)
        real_part = product[0, :, :half] - product[1, :, half:]
        imag_part = product[0, :, half:] + product[1, :, :half]
    return jnp.concatenate([real_part, imag_part], axis=1)


def matrix_product(left, right):
    product = jnp.einsum("cij,djk->cdik", left, right, preferred_element_type=jnp.float32)
    real_part = product[0, 0] - product[1, 1]
    imag_part = product[0, 1] + product[1, 0]
    return real_part, imag_part


def adjoint_product(left, right):
    product = jnp.einsum("ckj,dji->cdik", left, right, preferred_element_type=jnp.float32)
    real_part = product[0, 0] - product[1, 1]
    imag_part = -(product[0, 1] + product[1, 0])
    return real_part, imag_part


def stacked(columns):
    half = columns.shape[1] // 2
    return jnp.concatenate([columns[:, :half], columns[:, half:]], axis=0)


def joined(rows):
    half = rows.shape[0] // 2
    return jnp.concatenate([rows[:half], rows[half:]], axis=1)


def picked_rows(table, index):
    rows = table.shape[0]
    selector = (lax.broadcasted_iota(jnp.int32, (rows, index.shape[0]), 0) == index[None, :])
    return jnp.einsum(
        "ar,ap->rp", table, selector.astype(table.dtype), preferred_element_type=jnp.float32
    )


def sweeps(blocks, forward_src, backward_src):
    count = lax.axis_size("section")
    odd = lax.axis_index("section") % 2 == 1
    swap = [(2 * y + side, 2 * y + 1 - side) for y in range(count // 2) for side in (0, 1)]
    other_blocks, other_src = lax.ppermute(
        (blocks, jnp.where(odd, backward_src, forward_src)), "section", swap
    )
    left = jnp.where(odd, blocks, other_blocks)
    right = jnp.where(odd, other_blocks, blocks)
    forward_real, forward_imag = matrix_product(left, right)
    backward_real, backward_imag = adjoint_product(left, right)
    real_part = jnp.where(odd, forward_real, backward_real).astype(jnp.bfloat16)
    imag_part = jnp.where(odd, forward_imag, backward_imag).astype(jnp.bfloat16)
    pair_forward = (complex_product(blocks, other_src, False) + forward_src).astype(jnp.bfloat16)
    pair_backward = (complex_product(blocks, other_src, True) + backward_src).astype(jnp.bfloat16)
    chain_src = stacked(jnp.where(odd, pair_forward, pair_backward))
    chips = count // 2
    chip = lax.axis_index("section") // 2
    chain = [(2 * y + 1, 2 * y + 3) for y in range(chips - 1)]
    chain += [(2 * y, 2 * y - 2) for y in range(1, chips)]
    own_map = jnp.stack([real_part, imag_part])
    upstream_map, upstream_src = lax.ppermute((own_map, chain_src), "section", chain)
    has_upstream = jnp.where(odd, chip >= 1, chip <= chips - 2)
    joint_real, joint_imag = matrix_product(own_map, upstream_map)
    joint_real = jnp.where(has_upstream, joint_real, real_part).astype(jnp.bfloat16)
    joint_imag = jnp.where(has_upstream, joint_imag, imag_part).astype(jnp.bfloat16)
    joint_src = (stacked(complex_product(own_map, joined(upstream_src), False))
                 + chain_src).astype(jnp.bfloat16)
    joint_map = jnp.concatenate(
        [
            jnp.concatenate([joint_real, -joint_imag], axis=1),
            jnp.concatenate([joint_imag, joint_real], axis=1),
        ],
        axis=0,
    )
    stride = [(2 * y + 1, 2 * y + 5) for y in range(chips - 2)]
    stride += [(2 * y, 2 * y - 4) for y in range(2, chips)]
    state = joint_src
    for _ in range((chips - 1) // 2):
        arrived = lax.ppermute(state, "section", stride)
        state = (jnp.dot(joint_map, arrived, preferred_element_type=jnp.float32)
                 + joint_src).astype(jnp.bfloat16)
    state = joined(state)
    hand_over = [(s, s + 1) for s in range(1, count - 1, 2)]
    hand_over += [(s, s - 1) for s in range(2, count, 2)]
    neighbour = lax.ppermute(state, "section", hand_over)
    fields = jnp.where(
        odd, state, (complex_product(blocks, neighbour, False) + forward_src).astype(jnp.bfloat16)
    )
    adjoints = jnp.where(
        odd, (complex_product(blocks, neighbour, True) + backward_src).astype(jnp.bfloat16), state
    )
    return fields, adjoints


SHIFT_ROUNDS = (((1, (0,)), (2, (0,))), ((3, (0, 1)), (4, (1, 2))))


def shifted_copies(sent, direction):
    copies = {0: sent}
    for rounds in SHIFT_ROUNDS:
        arrived = {}
        for step, held in rounds:
            payload = jnp.stack([copies[k] for k in held])
            moved = passed_along(payload, "energy", direction * step)
            for j, k in enumerate(held):
                arrived[k + step] = moved[j]
        copies.update(arrived)
    return copies


def on_device(
    propagator, forward_source, backward_source, left_orbital, right_orbital, phonon_shift, coupling
):
    orbitals = propagator.shape[3]
    modes = forward_source.shape[3] // 2
    fields, adjoints = sweeps(propagator[0, 0], forward_source[0, 0], backward_source[0, 0])

    section_base = lax.axis_index("section") * orbitals
    left_rows = picked_rows(fields, left_orbital - section_base)
    right_rows = picked_rows(adjoints, right_orbital - section_base)
    real_part = jnp.sum(left_rows * right_rows, axis=0)
    imag_part = jnp.sum(left_rows[modes:] * right_rows[:modes], axis=0) - jnp.sum(
        left_rows[:modes] * right_rows[modes:], axis=0
    )
    lesser_part = jnp.stack([real_part, imag_part]) * modes ** (-0.5)

    sent = lesser_part.astype(jnp.bfloat16)
    moved = {0: lesser_part}
    for direction in (1, -1):
        for k, copy in shifted_copies(sent, direction).items():
            if k != 0:
                moved[direction * k] = copy.astype(jnp.float32)
    self_energy = jnp.zeros_like(lesser_part)
    for offset in range(-MAX_SHIFT, MAX_SHIFT + 1):
        weight = jnp.sum(jnp.where((phonon_shift == offset)[:, None], coupling, 0.0), axis=0)
        self_energy = self_energy + weight[None, :] * moved[offset]
    return self_energy[:, None, :]


def solution(mesh):
    placed = (
        P("energy", "section", None, None, None),
        P("energy", "section", None, None),
        P("energy", "section", None, None),
        P("section"),
        P("section"),
        P(),
        P(None, "section"),
    )
    return jax.shard_map(
        on_device,
        mesh=mesh,
        in_specs=placed,
        out_specs=P(None, "energy", "section"),
        check_vma=False,
    )
```

```python
import jax
import jax.numpy as jnp
from jax import lax
from jax.sharding import PartitionSpec as P

MAX_SHIFT = 6


def passed_along(value, axis, steps):
    count = lax.axis_size(axis)
    leading, last = (max(0, -steps), min(count, count - steps))
    return lax.ppermute(value, axis, [(source, source + steps) for source in range(leading, last)])


def complex_product(matrix, columns, adjoint):
    half = columns.shape[1] // 2
    if adjoint:
        product = jnp.einsum("cji,jn->cin", matrix, columns, preferred_element_type=jnp.float32)
        real_part = product[0, :, :half] + product[1, :, half:]
        imag_part = product[0, :, half:] - product[1, :, :half]
    else:
        product = jnp.einsum("cij,jn->cin", matrix, columns, preferred_element_type=jnp.float32)
        real_part = product[0, :, :half] - product[1, :, half:]
        imag_part = product[0, :, half:] + product[1, :, :half]
    return jnp.concatenate([real_part, imag_part], axis=1)


def matrix_product(left, right):
    product = jnp.einsum("cij,djk->cdik", left, right, preferred_element_type=jnp.float32)
    real_part = product[0, 0] - product[1, 1]
    imag_part = product[0, 1] + product[1, 0]
    return real_part, imag_part


def adjoint_product(left, right):
    product = jnp.einsum("ckj,dji->cdik", left, right, preferred_element_type=jnp.float32)
    real_part = product[0, 0] - product[1, 1]
    imag_part = -(product[0, 1] + product[1, 0])
    return real_part, imag_part


def stacked(columns):
    half = columns.shape[1] // 2
    return jnp.concatenate([columns[:, :half], columns[:, half:]], axis=0)


def joined(rows):
    half = rows.shape[0] // 2
    return jnp.concatenate([rows[:half], rows[half:]], axis=1)


def picked_rows(table, index):
    rows = table.shape[0]
    selector = (lax.broadcasted_iota(jnp.int32, (rows, index.shape[0]), 0) == index[None, :])
    return jnp.einsum(
        "ar,ap->rp", table, selector.astype(table.dtype), preferred_element_type=jnp.float32
    )


def sweeps(blocks, forward_src, backward_src):
    count = lax.axis_size("section")
    odd = lax.axis_index("section") % 2 == 1
    swap = [(2 * y + side, 2 * y + 1 - side) for y in range(count // 2) for side in (0, 1)]
    other_blocks, other_src = lax.ppermute(
        (blocks, jnp.where(odd, backward_src, forward_src)), "section", swap
    )
    left = jnp.where(odd, blocks, other_blocks)
    right = jnp.where(odd, other_blocks, blocks)
    forward_real, forward_imag = matrix_product(left, right)
    backward_real, backward_imag = adjoint_product(left, right)
    real_part = jnp.where(odd, forward_real, backward_real).astype(jnp.bfloat16)
    imag_part = jnp.where(odd, forward_imag, backward_imag).astype(jnp.bfloat16)
    pair_forward = (complex_product(blocks, other_src, False) + forward_src).astype(jnp.bfloat16)
    pair_backward = (complex_product(blocks, other_src, True) + backward_src).astype(jnp.bfloat16)
    chain_src = stacked(jnp.where(odd, pair_forward, pair_backward))
    chips = count // 2
    chip = lax.axis_index("section") // 2
    chain = [(2 * y + 1, 2 * y + 3) for y in range(chips - 1)]
    chain += [(2 * y, 2 * y - 2) for y in range(1, chips)]
    own_map = jnp.stack([real_part, imag_part])
    upstream_map, upstream_src = lax.ppermute((own_map, chain_src), "section", chain)
    has_upstream = jnp.where(odd, chip >= 1, chip <= chips - 2)
    joint_real, joint_imag = matrix_product(own_map, upstream_map)
    joint_real = jnp.where(has_upstream, joint_real, real_part).astype(jnp.bfloat16)
    joint_imag = jnp.where(has_upstream, joint_imag, imag_part).astype(jnp.bfloat16)
    joint_src = (stacked(complex_product(own_map, joined(upstream_src), False))
                 + chain_src).astype(jnp.bfloat16)
    joint_map = jnp.concatenate(
        [
            jnp.concatenate([joint_real, -joint_imag], axis=1),
            jnp.concatenate([joint_imag, joint_real], axis=1),
        ],
        axis=0,
    )
    stride = [(2 * y + 1, 2 * y + 5) for y in range(chips - 2)]
    stride += [(2 * y, 2 * y - 4) for y in range(2, chips)]
    state = joint_src
    for _ in range((chips - 1) // 2):
        arrived = lax.ppermute(state, "section", stride)
        state = (jnp.dot(joint_map, arrived, preferred_element_type=jnp.float32)
                 + joint_src).astype(jnp.bfloat16)
    state = joined(state)
    hand_over = [(s, s + 1) for s in range(1, count - 1, 2)]
    hand_over += [(s, s - 1) for s in range(2, count, 2)]
    neighbour = lax.ppermute(state, "section", hand_over)
    fields = jnp.where(
        odd, state, (complex_product(blocks, neighbour, False) + forward_src).astype(jnp.bfloat16)
    )
    adjoints = jnp.where(
        odd, (complex_product(blocks, neighbour, True) + backward_src).astype(jnp.bfloat16), state
    )
    return fields, adjoints


SHIFT_ROUNDS = (tuple((step, (0,)) for step in range(1, MAX_SHIFT + 1)),)


def shifted_copies(sent, direction):
    copies = {0: sent}
    for rounds in SHIFT_ROUNDS:
        arrived = {}
        for step, held in rounds:
            payload = jnp.stack([copies[k] for k in held])
            moved = passed_along(payload, "energy", direction * step)
            for j, k in enumerate(held):
                arrived[k + step] = moved[j]
        copies.update(arrived)
    return copies


def on_device(
    propagator, forward_source, backward_source, left_orbital, right_orbital, phonon_shift, coupling
):
    orbitals = propagator.shape[3]
    modes = forward_source.shape[3] // 2
    fields, adjoints = sweeps(propagator[0, 0], forward_source[0, 0], backward_source[0, 0])

    section_base = lax.axis_index("section") * orbitals
    left_rows = picked_rows(fields, left_orbital - section_base)
    right_rows = picked_rows(adjoints, right_orbital - section_base)
    real_part = jnp.sum(left_rows * right_rows, axis=0)
    imag_part = jnp.sum(left_rows[modes:] * right_rows[:modes], axis=0) - jnp.sum(
        left_rows[:modes] * right_rows[modes:], axis=0
    )
    lesser_part = jnp.stack([real_part, imag_part]) * modes ** (-0.5)

    sent = lesser_part.astype(jnp.bfloat16)
    moved = {0: lesser_part}
    for direction in (1, -1):
        for k, copy in shifted_copies(sent, direction).items():
            if k != 0:
                moved[direction * k] = copy.astype(jnp.float32)
    self_energy = jnp.zeros_like(lesser_part)
    for offset in range(-MAX_SHIFT, MAX_SHIFT + 1):
        weight = jnp.sum(jnp.where((phonon_shift == offset)[:, None], coupling, 0.0), axis=0)
        self_energy = self_energy + weight[None, :] * moved[offset]
    return self_energy[:, None, :]


def solution(mesh):
    placed = (
        P("energy", "section", None, None, None),
        P("energy", "section", None, None),
        P("energy", "section", None, None),
        P("section"),
        P("section"),
        P(),
        P(None, "section"),
    )
    return jax.shard_map(
        on_device,
        mesh=mesh,
        in_specs=placed,
        out_specs=P(None, "energy", "section"),
        check_vma=False,
    )
```

```python
import jax
import jax.numpy as jnp
from jax import lax
from jax.sharding import PartitionSpec as P

MAX_SHIFT = 6


def passed_along(value, axis, steps):
    count = lax.axis_size(axis)
    leading, last = (max(0, -steps), min(count, count - steps))
    return lax.ppermute(value, axis, [(source, source + steps) for source in range(leading, last)])


def complex_product(matrix, columns, adjoint):
    half = columns.shape[1] // 2
    if adjoint:
        product = jnp.einsum("cji,jn->cin", matrix, columns, preferred_element_type=jnp.float32)
        real_part = product[0, :, :half] + product[1, :, half:]
        imag_part = product[0, :, half:] - product[1, :, :half]
    else:
        product = jnp.einsum("cij,jn->cin", matrix, columns, preferred_element_type=jnp.float32)
        real_part = product[0, :, :half] - product[1, :, half:]
        imag_part = product[0, :, half:] + product[1, :, :half]
    return jnp.concatenate([real_part, imag_part], axis=1)


def matrix_product(left, right):
    product = jnp.einsum("cij,djk->cdik", left, right, preferred_element_type=jnp.float32)
    real_part = product[0, 0] - product[1, 1]
    imag_part = product[0, 1] + product[1, 0]
    return real_part, imag_part


def adjoint_product(left, right):
    product = jnp.einsum("ckj,dji->cdik", left, right, preferred_element_type=jnp.float32)
    real_part = product[0, 0] - product[1, 1]
    imag_part = -(product[0, 1] + product[1, 0])
    return real_part, imag_part


def stacked(columns):
    half = columns.shape[1] // 2
    return jnp.concatenate([columns[:, :half], columns[:, half:]], axis=0)


def joined(rows):
    half = rows.shape[0] // 2
    return jnp.concatenate([rows[:half], rows[half:]], axis=1)


def picked_rows(table, index):
    rows = table.shape[0]
    selector = (lax.broadcasted_iota(jnp.int32, (rows, index.shape[0]), 0) == index[None, :])
    return jnp.einsum(
        "ar,ap->rp", table, selector.astype(table.dtype), preferred_element_type=jnp.float32
    )


def packed(pair, columns):
    return jnp.concatenate([pair[0], pair[1], columns], axis=1)


def unpacked(joined_array):
    width = joined_array.shape[0]
    pair = jnp.stack([joined_array[:, :width], joined_array[:, width:2 * width]])
    return pair, joined_array[:, 2 * width:]


def sweeps(blocks, forward_src, backward_src):
    count = lax.axis_size("section")
    odd = lax.axis_index("section") % 2 == 1
    swap = [(2 * y + side, 2 * y + 1 - side) for y in range(count // 2) for side in (0, 1)]
    other_blocks, other_src = unpacked(
        lax.ppermute(packed(blocks, jnp.where(odd, backward_src, forward_src)), "section", swap)
    )
    left = jnp.where(odd, blocks, other_blocks)
    right = jnp.where(odd, other_blocks, blocks)
    forward_real, forward_imag = matrix_product(left, right)
    backward_real, backward_imag = adjoint_product(left, right)
    real_part = jnp.where(odd, forward_real, backward_real).astype(jnp.bfloat16)
    imag_part = jnp.where(odd, forward_imag, backward_imag).astype(jnp.bfloat16)
    pair_forward = (complex_product(blocks, other_src, False) + forward_src).astype(jnp.bfloat16)
    pair_backward = (complex_product(blocks, other_src, True) + backward_src).astype(jnp.bfloat16)
    chain_src = jnp.where(odd, pair_forward, pair_backward)
    chips = count // 2
    chip = lax.axis_index("section") // 2
    chain = [(2 * y + 1, 2 * y + 3) for y in range(chips - 1)]
    chain += [(2 * y, 2 * y - 2) for y in range(1, chips)]
    own_map = jnp.stack([real_part, imag_part])
    upstream_map, upstream_src = unpacked(
        lax.ppermute(packed(own_map, chain_src), "section", chain)
    )
    has_upstream = jnp.where(odd, chip >= 1, chip <= chips - 2)
    joint_real, joint_imag = matrix_product(own_map, upstream_map)
    joint_real = jnp.where(has_upstream, joint_real, real_part).astype(jnp.bfloat16)
    joint_imag = jnp.where(has_upstream, joint_imag, imag_part).astype(jnp.bfloat16)
    joint_src = stacked(
        (complex_product(own_map, upstream_src, False) + chain_src).astype(jnp.bfloat16)
    )
    joint_map = jnp.concatenate(
        [
            jnp.concatenate([joint_real, -joint_imag], axis=1),
            jnp.concatenate([joint_imag, joint_real], axis=1),
        ],
        axis=0,
    )
    stride = [(2 * y + 1, 2 * y + 5) for y in range(chips - 2)]
    stride += [(2 * y, 2 * y - 4) for y in range(2, chips)]
    state = joint_src
    for _ in range((chips - 1) // 2):
        arrived = lax.ppermute(state, "section", stride)
        state = (jnp.dot(joint_map, arrived, preferred_element_type=jnp.float32)
                 + joint_src).astype(jnp.bfloat16)
    state = joined(state)
    hand_over = [(s, s + 1) for s in range(1, count - 1, 2)]
    hand_over += [(s, s - 1) for s in range(2, count, 2)]
    neighbour = lax.ppermute(state, "section", hand_over)
    fields = jnp.where(
        odd, state, (complex_product(blocks, neighbour, False) + forward_src).astype(jnp.bfloat16)
    )
    adjoints = jnp.where(
        odd, (complex_product(blocks, neighbour, True) + backward_src).astype(jnp.bfloat16), state
    )
    return fields, adjoints


SHIFT_ROUNDS = (((1, (0,)), (2, (0,))), ((3, (0, 1)), (4, (1, 2))))


def shifted_copies(sent, direction):
    copies = {0: sent}
    for rounds in SHIFT_ROUNDS:
        arrived = {}
        for step, held in rounds:
            payload = jnp.stack([copies[k] for k in held])
            moved = passed_along(payload, "energy", direction * step)
            for j, k in enumerate(held):
                arrived[k + step] = moved[j]
        copies.update(arrived)
    return copies


def on_device(
    propagator, forward_source, backward_source, left_orbital, right_orbital, phonon_shift, coupling
):
    orbitals = propagator.shape[3]
    modes = forward_source.shape[3] // 2
    fields, adjoints = sweeps(propagator[0, 0], forward_source[0, 0], backward_source[0, 0])

    section_base = lax.axis_index("section") * orbitals
    left_rows = picked_rows(fields, left_orbital - section_base)
    right_rows = picked_rows(adjoints, right_orbital - section_base)
    real_part = jnp.sum(left_rows * right_rows, axis=0)
    imag_part = jnp.sum(left_rows[modes:] * right_rows[:modes], axis=0) - jnp.sum(
        left_rows[:modes] * right_rows[modes:], axis=0
    )
    lesser_part = jnp.stack([real_part, imag_part]) * modes ** (-0.5)

    sent = lesser_part.astype(jnp.bfloat16)
    moved = {0: lesser_part}
    for direction in (1, -1):
        for k, copy in shifted_copies(sent, direction).items():
            if k != 0:
                moved[direction * k] = copy.astype(jnp.float32)
    self_energy = jnp.zeros_like(lesser_part)
    for offset in range(-MAX_SHIFT, MAX_SHIFT + 1):
        weight = jnp.sum(jnp.where((phonon_shift == offset)[:, None], coupling, 0.0), axis=0)
        self_energy = self_energy + weight[None, :] * moved[offset]
    return self_energy[:, None, :]


def solution(mesh):
    placed = (
        P("energy", "section", None, None, None),
        P("energy", "section", None, None),
        P("energy", "section", None, None),
        P("section"),
        P("section"),
        P(),
        P(None, "section"),
    )
    return jax.shard_map(
        on_device,
        mesh=mesh,
        in_specs=placed,
        out_specs=P(None, "energy", "section"),
        check_vma=False,
    )
```

```python
import jax
import jax.numpy as jnp
from jax import lax
from jax.sharding import PartitionSpec as P

MAX_SHIFT = 6


def passed_along(value, axis, steps):
    count = lax.axis_size(axis)
    leading, last = (max(0, -steps), min(count, count - steps))
    return lax.ppermute(value, axis, [(source, source + steps) for source in range(leading, last)])


def complex_product(matrix, columns, adjoint):
    half = columns.shape[1] // 2
    if adjoint:
        product = jnp.einsum("cji,jn->cin", matrix, columns, preferred_element_type=jnp.float32)
        real_part = product[0, :, :half] + product[1, :, half:]
        imag_part = product[0, :, half:] - product[1, :, :half]
    else:
        product = jnp.einsum("cij,jn->cin", matrix, columns, preferred_element_type=jnp.float32)
        real_part = product[0, :, :half] - product[1, :, half:]
        imag_part = product[0, :, half:] + product[1, :, :half]
    return jnp.concatenate([real_part, imag_part], axis=1)


def matrix_product(left, right):
    product = jnp.einsum("cij,djk->cdik", left, right, preferred_element_type=jnp.float32)
    real_part = product[0, 0] - product[1, 1]
    imag_part = product[0, 1] + product[1, 0]
    return real_part, imag_part


def adjoint_product(left, right):
    product = jnp.einsum("ckj,dji->cdik", left, right, preferred_element_type=jnp.float32)
    real_part = product[0, 0] - product[1, 1]
    imag_part = -(product[0, 1] + product[1, 0])
    return real_part, imag_part


def stacked(columns):
    half = columns.shape[1] // 2
    return jnp.concatenate([columns[:, :half], columns[:, half:]], axis=0)


def joined(rows):
    half = rows.shape[0] // 2
    return jnp.concatenate([rows[:half], rows[half:]], axis=1)


def picked_rows(table, index):
    rows = table.shape[0]
    selector = (lax.broadcasted_iota(jnp.int32, (rows, index.shape[0]), 0) == index[None, :])
    return jnp.einsum(
        "ar,ap->rp", table, selector.astype(table.dtype), preferred_element_type=jnp.float32
    )


def sweeps(blocks, forward_src, backward_src):
    count = lax.axis_size("section")
    odd = lax.axis_index("section") % 2 == 1
    swap = [(2 * y + side, 2 * y + 1 - side) for y in range(count // 2) for side in (0, 1)]
    other_blocks, other_src = lax.ppermute(
        (blocks, jnp.where(odd, backward_src, forward_src)), "section", swap
    )
    left = jnp.where(odd, blocks, other_blocks)
    right = jnp.where(odd, other_blocks, blocks)
    forward_real, forward_imag = matrix_product(left, right)
    backward_real, backward_imag = adjoint_product(left, right)
    real_part = jnp.where(odd, forward_real, backward_real).astype(jnp.bfloat16)
    imag_part = jnp.where(odd, forward_imag, backward_imag).astype(jnp.bfloat16)
    pair_forward = (complex_product(blocks, other_src, False) + forward_src).astype(jnp.bfloat16)
    pair_backward = (complex_product(blocks, other_src, True) + backward_src).astype(jnp.bfloat16)
    chain_src = stacked(jnp.where(odd, pair_forward, pair_backward))
    chips = count // 2
    chip = lax.axis_index("section") // 2
    chain = [(2 * y + 1, 2 * y + 3) for y in range(chips - 1)]
    chain += [(2 * y, 2 * y - 2) for y in range(1, chips)]
    own_map = jnp.stack([real_part, imag_part])
    upstream_map, upstream_src = lax.ppermute((own_map, chain_src), "section", chain)
    has_upstream = jnp.where(odd, chip >= 1, chip <= chips - 2)
    joint_real, joint_imag = matrix_product(own_map, upstream_map)
    joint_real = jnp.where(has_upstream, joint_real, real_part).astype(jnp.bfloat16)
    joint_imag = jnp.where(has_upstream, joint_imag, imag_part).astype(jnp.bfloat16)
    joint_src = (stacked(complex_product(own_map, joined(upstream_src), False))
                 + chain_src).astype(jnp.bfloat16)
    joint_map = jnp.concatenate(
        [
            jnp.concatenate([joint_real, -joint_imag], axis=1),
            jnp.concatenate([joint_imag, joint_real], axis=1),
        ],
        axis=0,
    )
    stride = [(2 * y + 1, 2 * y + 5) for y in range(chips - 2)]
    stride += [(2 * y, 2 * y - 4) for y in range(2, chips)]
    state = joint_src
    for _ in range((chips - 1) // 2):
        arrived = lax.ppermute(state, "section", stride)
        state = (jnp.dot(joint_map, arrived, preferred_element_type=jnp.float32)
                 + joint_src).astype(jnp.bfloat16)
    state = joined(state)
    hand_over = [(s, s + 1) for s in range(1, count - 1, 2)]
    hand_over += [(s, s - 1) for s in range(2, count, 2)]
    neighbour = lax.ppermute(state, "section", hand_over)
    other = jnp.where(
        odd,
        (complex_product(blocks, neighbour, True) + backward_src).astype(jnp.bfloat16),
        (complex_product(blocks, neighbour, False) + forward_src).astype(jnp.bfloat16),
    )
    return state, other


SHIFT_ROUNDS = (((1, (0,)), (2, (0,))), ((3, (0, 1)), (4, (1, 2))))


def shifted_copies(sent, direction):
    copies = {0: sent}
    for rounds in SHIFT_ROUNDS:
        arrived = {}
        for step, held in rounds:
            payload = jnp.stack([copies[k] for k in held])
            moved = passed_along(payload, "energy", direction * step)
            for j, k in enumerate(held):
                arrived[k + step] = moved[j]
        copies.update(arrived)
    return copies


def on_device(
    propagator, forward_source, backward_source, left_orbital, right_orbital, phonon_shift, coupling
):
    orbitals = propagator.shape[3]
    modes = forward_source.shape[3] // 2
    own, other = sweeps(propagator[0, 0], forward_source[0, 0], backward_source[0, 0])
    odd = lax.axis_index("section") % 2 == 1
    section_base = lax.axis_index("section") * orbitals
    left_local = left_orbital - section_base
    right_local = right_orbital - section_base
    own_rows = picked_rows(own, jnp.where(odd, left_local, right_local))
    other_rows = picked_rows(other, jnp.where(odd, right_local, left_local))
    real_part = jnp.sum(own_rows * other_rows, axis=0)
    swapped_imag = jnp.sum(own_rows[modes:] * other_rows[:modes], axis=0) - jnp.sum(
        own_rows[:modes] * other_rows[modes:], axis=0
    )
    imag_part = jnp.where(odd, swapped_imag, -swapped_imag)
    lesser_part = jnp.stack([real_part, imag_part]) * modes ** (-0.5)

    sent = lesser_part.astype(jnp.bfloat16)
    moved = {0: lesser_part}
    for direction in (1, -1):
        for k, copy in shifted_copies(sent, direction).items():
            if k != 0:
                moved[direction * k] = copy.astype(jnp.float32)
    self_energy = jnp.zeros_like(lesser_part)
    for offset in range(-MAX_SHIFT, MAX_SHIFT + 1):
        weight = jnp.sum(jnp.where((phonon_shift == offset)[:, None], coupling, 0.0), axis=0)
        self_energy = self_energy + weight[None, :] * moved[offset]
    return self_energy[:, None, :]


def solution(mesh):
    placed = (
        P("energy", "section", None, None, None),
        P("energy", "section", None, None),
        P("energy", "section", None, None),
        P("section"),
        P("section"),
        P(),
        P(None, "section"),
    )
    return jax.shard_map(
        on_device,
        mesh=mesh,
        in_specs=placed,
        out_specs=P(None, "energy", "section"),
        check_vma=False,
    )
```

```python
import jax
import jax.numpy as jnp
from jax import lax
from jax.sharding import PartitionSpec as P

MAX_SHIFT = 6


def passed_along(value, axis, steps):
    count = lax.axis_size(axis)
    leading, last = (max(0, -steps), min(count, count - steps))
    return lax.ppermute(value, axis, [(source, source + steps) for source in range(leading, last)])


def complex_product(matrix, columns, adjoint):
    half = columns.shape[1] // 2
    if adjoint:
        product = jnp.einsum("cji,jn->cin", matrix, columns, preferred_element_type=jnp.float32)
        real_part = product[0, :, :half] + product[1, :, half:]
        imag_part = product[0, :, half:] - product[1, :, :half]
    else:
        product = jnp.einsum("cij,jn->cin", matrix, columns, preferred_element_type=jnp.float32)
        real_part = product[0, :, :half] - product[1, :, half:]
        imag_part = product[0, :, half:] + product[1, :, :half]
    return jnp.concatenate([real_part, imag_part], axis=1)


def matrix_product(left, right):
    product = jnp.einsum("cij,djk->cdik", left, right, preferred_element_type=jnp.float32)
    real_part = product[0, 0] - product[1, 1]
    imag_part = product[0, 1] + product[1, 0]
    return real_part, imag_part


def adjoint_product(left, right):
    product = jnp.einsum("ckj,dji->cdik", left, right, preferred_element_type=jnp.float32)
    real_part = product[0, 0] - product[1, 1]
    imag_part = -(product[0, 1] + product[1, 0])
    return real_part, imag_part


def stacked(columns):
    half = columns.shape[1] // 2
    return jnp.concatenate([columns[:, :half], columns[:, half:]], axis=0)


def joined(rows):
    half = rows.shape[0] // 2
    return jnp.concatenate([rows[:half], rows[half:]], axis=1)


def picked_rows(table, index):
    rows = table.shape[0]
    selector = (lax.broadcasted_iota(jnp.int32, (rows, index.shape[0]), 0) == index[None, :])
    return jnp.einsum(
        "ar,ap->rp", table, selector.astype(table.dtype), preferred_element_type=jnp.float32
    )


def sweeps(blocks, forward_src, backward_src):
    count = lax.axis_size("section")
    odd = lax.axis_index("section") % 2 == 1
    swap = [(2 * y + side, 2 * y + 1 - side) for y in range(count // 2) for side in (0, 1)]
    other_blocks, other_src = lax.ppermute(
        (blocks, jnp.where(odd, backward_src, forward_src)), "section", swap
    )

    def forward_pair():
        real_part, imag_part = matrix_product(blocks, other_blocks)
        source = complex_product(blocks, other_src, False) + forward_src
        return real_part.astype(jnp.bfloat16), imag_part.astype(jnp.bfloat16), source.astype(
            jnp.bfloat16
        )

    def backward_pair():
        real_part, imag_part = adjoint_product(other_blocks, blocks)
        source = complex_product(blocks, other_src, True) + backward_src
        return real_part.astype(jnp.bfloat16), imag_part.astype(jnp.bfloat16), source.astype(
            jnp.bfloat16
        )

    real_part, imag_part, pair_src = lax.cond(odd, forward_pair, backward_pair)
    chain_src = stacked(pair_src)
    chips = count // 2
    chip = lax.axis_index("section") // 2
    chain = [(2 * y + 1, 2 * y + 3) for y in range(chips - 1)]
    chain += [(2 * y, 2 * y - 2) for y in range(1, chips)]
    own_map = jnp.stack([real_part, imag_part])
    upstream_map, upstream_src = lax.ppermute((own_map, chain_src), "section", chain)
    has_upstream = jnp.where(odd, chip >= 1, chip <= chips - 2)
    joint_real, joint_imag = matrix_product(own_map, upstream_map)
    joint_real = jnp.where(has_upstream, joint_real, real_part).astype(jnp.bfloat16)
    joint_imag = jnp.where(has_upstream, joint_imag, imag_part).astype(jnp.bfloat16)
    joint_src = (stacked(complex_product(own_map, joined(upstream_src), False))
                 + chain_src).astype(jnp.bfloat16)
    joint_map = jnp.concatenate(
        [
            jnp.concatenate([joint_real, -joint_imag], axis=1),
            jnp.concatenate([joint_imag, joint_real], axis=1),
        ],
        axis=0,
    )
    stride = [(2 * y + 1, 2 * y + 5) for y in range(chips - 2)]
    stride += [(2 * y, 2 * y - 4) for y in range(2, chips)]
    state = joint_src
    for _ in range((chips - 1) // 2):
        arrived = lax.ppermute(state, "section", stride)
        state = (jnp.dot(joint_map, arrived, preferred_element_type=jnp.float32)
                 + joint_src).astype(jnp.bfloat16)
    state = joined(state)
    hand_over = [(s, s + 1) for s in range(1, count - 1, 2)]
    hand_over += [(s, s - 1) for s in range(2, count, 2)]
    neighbour = lax.ppermute(state, "section", hand_over)
    other = jnp.where(
        odd,
        (complex_product(blocks, neighbour, True) + backward_src).astype(jnp.bfloat16),
        (complex_product(blocks, neighbour, False) + forward_src).astype(jnp.bfloat16),
    )
    return state, other


SHIFT_ROUNDS = (((1, (0,)), (2, (0,))), ((3, (0, 1)), (4, (1, 2))))


def shifted_copies(sent, direction):
    copies = {0: sent}
    for rounds in SHIFT_ROUNDS:
        arrived = {}
        for step, held in rounds:
            payload = jnp.stack([copies[k] for k in held])
            moved = passed_along(payload, "energy", direction * step)
            for j, k in enumerate(held):
                arrived[k + step] = moved[j]
        copies.update(arrived)
    return copies


def on_device(
    propagator, forward_source, backward_source, left_orbital, right_orbital, phonon_shift, coupling
):
    orbitals = propagator.shape[3]
    modes = forward_source.shape[3] // 2
    own, other = sweeps(propagator[0, 0], forward_source[0, 0], backward_source[0, 0])
    odd = lax.axis_index("section") % 2 == 1
    section_base = lax.axis_index("section") * orbitals
    left_local = left_orbital - section_base
    right_local = right_orbital - section_base
    own_rows = picked_rows(own, jnp.where(odd, left_local, right_local))
    other_rows = picked_rows(other, jnp.where(odd, right_local, left_local))
    real_part = jnp.sum(own_rows * other_rows, axis=0)
    swapped_imag = jnp.sum(own_rows[modes:] * other_rows[:modes], axis=0) - jnp.sum(
        own_rows[:modes] * other_rows[modes:], axis=0
    )
    imag_part = jnp.where(odd, swapped_imag, -swapped_imag)
    lesser_part = jnp.stack([real_part, imag_part]) * modes ** (-0.5)

    sent = lesser_part.astype(jnp.bfloat16)
    moved = {0: lesser_part}
    for direction in (1, -1):
        for k, copy in shifted_copies(sent, direction).items():
            if k != 0:
                moved[direction * k] = copy.astype(jnp.float32)
    self_energy = jnp.zeros_like(lesser_part)
    for offset in range(-MAX_SHIFT, MAX_SHIFT + 1):
        weight = jnp.sum(jnp.where((phonon_shift == offset)[:, None], coupling, 0.0), axis=0)
        self_energy = self_energy + weight[None, :] * moved[offset]
    return self_energy[:, None, :]


def solution(mesh):
    placed = (
        P("energy", "section", None, None, None),
        P("energy", "section", None, None),
        P("energy", "section", None, None),
        P("section"),
        P("section"),
        P(),
        P(None, "section"),
    )
    return jax.shard_map(
        on_device,
        mesh=mesh,
        in_specs=placed,
        out_specs=P(None, "energy", "section"),
        check_vma=False,
    )
```

```python
import jax
import jax.numpy as jnp
from jax import lax
from jax.sharding import PartitionSpec as P

MAX_SHIFT = 6


def passed_along(value, axis, steps):
    count = lax.axis_size(axis)
    leading, last = (max(0, -steps), min(count, count - steps))
    return lax.ppermute(value, axis, [(source, source + steps) for source in range(leading, last)])


def complex_product(matrix, columns, adjoint):
    half = columns.shape[1] // 2
    if adjoint:
        product = jnp.einsum("cji,jn->cin", matrix, columns, preferred_element_type=jnp.float32)
        real_part = product[0, :, :half] + product[1, :, half:]
        imag_part = product[0, :, half:] - product[1, :, :half]
    else:
        product = jnp.einsum("cij,jn->cin", matrix, columns, preferred_element_type=jnp.float32)
        real_part = product[0, :, :half] - product[1, :, half:]
        imag_part = product[0, :, half:] + product[1, :, :half]
    return jnp.concatenate([real_part, imag_part], axis=1)


def matrix_product(left, right):
    product = jnp.einsum("cij,djk->cdik", left, right, preferred_element_type=jnp.float32)
    real_part = product[0, 0] - product[1, 1]
    imag_part = product[0, 1] + product[1, 0]
    return real_part, imag_part


def adjoint_product(left, right):
    product = jnp.einsum("ckj,dji->cdik", left, right, preferred_element_type=jnp.float32)
    real_part = product[0, 0] - product[1, 1]
    imag_part = -(product[0, 1] + product[1, 0])
    return real_part, imag_part


def stacked(columns):
    half = columns.shape[1] // 2
    return jnp.concatenate([columns[:, :half], columns[:, half:]], axis=0)


def joined(rows):
    half = rows.shape[0] // 2
    return jnp.concatenate([rows[:half], rows[half:]], axis=1)


def picked_rows(table, index):
    rows = table.shape[0]
    selector = (lax.broadcasted_iota(jnp.int32, (rows, index.shape[0]), 0) == index[None, :])
    return jnp.einsum(
        "ar,ap->rp", table, selector.astype(table.dtype), preferred_element_type=jnp.float32
    )


def sweeps(blocks, forward_src, backward_src):
    count = lax.axis_size("section")
    odd = lax.axis_index("section") % 2 == 1
    swap = [(2 * y + side, 2 * y + 1 - side) for y in range(count // 2) for side in (0, 1)]
    other_blocks, other_src = lax.ppermute(
        (blocks, jnp.where(odd, backward_src, forward_src)), "section", swap
    )

    def forward_pair():
        real_part, imag_part = matrix_product(blocks, other_blocks)
        source = complex_product(blocks, other_src, False) + forward_src
        return jnp.stack([real_part, imag_part]).astype(jnp.bfloat16), source.astype(jnp.bfloat16)

    def backward_pair():
        real_part, imag_part = adjoint_product(other_blocks, blocks)
        source = complex_product(blocks, other_src, True) + backward_src
        return jnp.stack([real_part, imag_part]).astype(jnp.bfloat16), source.astype(jnp.bfloat16)

    own_map, pair_src = lax.cond(odd, forward_pair, backward_pair)
    real_part, imag_part = own_map[0], own_map[1]
    chain_src = stacked(pair_src)
    chips = count // 2
    chip = lax.axis_index("section") // 2
    chain = [(2 * y + 1, 2 * y + 3) for y in range(chips - 1)]
    chain += [(2 * y, 2 * y - 2) for y in range(1, chips)]
    upstream_map, upstream_src = lax.ppermute((own_map, chain_src), "section", chain)
    has_upstream = jnp.where(odd, chip >= 1, chip <= chips - 2)
    joint_real, joint_imag = matrix_product(own_map, upstream_map)
    joint_real = jnp.where(has_upstream, joint_real, real_part).astype(jnp.bfloat16)
    joint_imag = jnp.where(has_upstream, joint_imag, imag_part).astype(jnp.bfloat16)
    joint_src = (stacked(complex_product(own_map, joined(upstream_src), False))
                 + chain_src).astype(jnp.bfloat16)
    joint_map = jnp.concatenate(
        [
            jnp.concatenate([joint_real, -joint_imag], axis=1),
            jnp.concatenate([joint_imag, joint_real], axis=1),
        ],
        axis=0,
    )
    stride = [(2 * y + 1, 2 * y + 5) for y in range(chips - 2)]
    stride += [(2 * y, 2 * y - 4) for y in range(2, chips)]
    state = joint_src
    for _ in range((chips - 1) // 2):
        arrived = lax.ppermute(state, "section", stride)
        state = (jnp.dot(joint_map, arrived, preferred_element_type=jnp.float32)
                 + joint_src).astype(jnp.bfloat16)
    state = joined(state)
    hand_over = [(s, s + 1) for s in range(1, count - 1, 2)]
    hand_over += [(s, s - 1) for s in range(2, count, 2)]
    neighbour = lax.ppermute(state, "section", hand_over)
    other = jnp.where(
        odd,
        (complex_product(blocks, neighbour, True) + backward_src).astype(jnp.bfloat16),
        (complex_product(blocks, neighbour, False) + forward_src).astype(jnp.bfloat16),
    )
    return state, other


SHIFT_ROUNDS = (((1, (0,)), (2, (0,))), ((3, (0, 1)), (4, (1, 2))))


def shifted_copies(sent, direction):
    copies = {0: sent}
    for rounds in SHIFT_ROUNDS:
        arrived = {}
        for step, held in rounds:
            payload = jnp.stack([copies[k] for k in held])
            moved = passed_along(payload, "energy", direction * step)
            for j, k in enumerate(held):
                arrived[k + step] = moved[j]
        copies.update(arrived)
    return copies


def on_device(
    propagator, forward_source, backward_source, left_orbital, right_orbital, phonon_shift, coupling
):
    orbitals = propagator.shape[3]
    modes = forward_source.shape[3] // 2
    own, other = sweeps(propagator[0, 0], forward_source[0, 0], backward_source[0, 0])
    odd = lax.axis_index("section") % 2 == 1
    section_base = lax.axis_index("section") * orbitals
    left_local = left_orbital - section_base
    right_local = right_orbital - section_base
    own_rows = picked_rows(own, jnp.where(odd, left_local, right_local))
    other_rows = picked_rows(other, jnp.where(odd, right_local, left_local))
    real_part = jnp.sum(own_rows * other_rows, axis=0)
    swapped_imag = jnp.sum(own_rows[modes:] * other_rows[:modes], axis=0) - jnp.sum(
        own_rows[:modes] * other_rows[modes:], axis=0
    )
    imag_part = jnp.where(odd, swapped_imag, -swapped_imag)
    lesser_part = jnp.stack([real_part, imag_part]) * modes ** (-0.5)

    sent = lesser_part.astype(jnp.bfloat16)
    moved = {0: lesser_part}
    for direction in (1, -1):
        for k, copy in shifted_copies(sent, direction).items():
            if k != 0:
                moved[direction * k] = copy.astype(jnp.float32)
    self_energy = jnp.zeros_like(lesser_part)
    for offset in range(-MAX_SHIFT, MAX_SHIFT + 1):
        weight = jnp.sum(jnp.where((phonon_shift == offset)[:, None], coupling, 0.0), axis=0)
        self_energy = self_energy + weight[None, :] * moved[offset]
    return self_energy[:, None, :]


def solution(mesh):
    placed = (
        P("energy", "section", None, None, None),
        P("energy", "section", None, None),
        P("energy", "section", None, None),
        P("section"),
        P("section"),
        P(),
        P(None, "section"),
    )
    return jax.shard_map(
        on_device,
        mesh=mesh,
        in_specs=placed,
        out_specs=P(None, "energy", "section"),
        check_vma=False,
    )
```

```python
import jax
import jax.numpy as jnp
from jax import lax
from jax.sharding import PartitionSpec as P

MAX_SHIFT = 6


def passed_along(value, axis, steps):
    count = lax.axis_size(axis)
    leading, last = (max(0, -steps), min(count, count - steps))
    return lax.ppermute(value, axis, [(source, source + steps) for source in range(leading, last)])


def complex_product(matrix, columns, adjoint):
    half = columns.shape[1] // 2
    if adjoint:
        product = jnp.einsum("cji,jn->cin", matrix, columns, preferred_element_type=jnp.float32)
        real_part = product[0, :, :half] + product[1, :, half:]
        imag_part = product[0, :, half:] - product[1, :, :half]
    else:
        product = jnp.einsum("cij,jn->cin", matrix, columns, preferred_element_type=jnp.float32)
        real_part = product[0, :, :half] - product[1, :, half:]
        imag_part = product[0, :, half:] + product[1, :, :half]
    return jnp.concatenate([real_part, imag_part], axis=1)


def matrix_product(left, right):
    product = jnp.einsum("cij,djk->cdik", left, right, preferred_element_type=jnp.float32)
    real_part = product[0, 0] - product[1, 1]
    imag_part = product[0, 1] + product[1, 0]
    return real_part, imag_part


def adjoint_product(left, right):
    product = jnp.einsum("ckj,dji->cdik", left, right, preferred_element_type=jnp.float32)
    real_part = product[0, 0] - product[1, 1]
    imag_part = -(product[0, 1] + product[1, 0])
    return real_part, imag_part


def stacked(columns):
    half = columns.shape[1] // 2
    return jnp.concatenate([columns[:, :half], columns[:, half:]], axis=0)


def joined(rows):
    half = rows.shape[0] // 2
    return jnp.concatenate([rows[:half], rows[half:]], axis=1)


def picked_rows(table, index):
    rows = table.shape[0]
    selector = (lax.broadcasted_iota(jnp.int32, (rows, index.shape[0]), 0) == index[None, :])
    return jnp.einsum(
        "ar,ap->rp", table, selector.astype(table.dtype), preferred_element_type=jnp.float32
    )


def sweeps(blocks, forward_src, backward_src):
    count = lax.axis_size("section")
    odd = lax.axis_index("section") % 2 == 1
    swap = [(2 * y + side, 2 * y + 1 - side) for y in range(count // 2) for side in (0, 1)]
    other_blocks, other_src = lax.ppermute(
        (blocks, jnp.where(odd, backward_src, forward_src)), "section", swap
    )

    def forward_pair():
        real_part, imag_part = matrix_product(blocks, other_blocks)
        source = complex_product(blocks, other_src, False) + forward_src
        return real_part.astype(jnp.bfloat16), imag_part.astype(jnp.bfloat16), source.astype(
            jnp.bfloat16
        )

    def backward_pair():
        real_part, imag_part = adjoint_product(other_blocks, blocks)
        source = complex_product(blocks, other_src, True) + backward_src
        return real_part.astype(jnp.bfloat16), imag_part.astype(jnp.bfloat16), source.astype(
            jnp.bfloat16
        )

    real_part, imag_part, pair_src = lax.cond(odd, forward_pair, backward_pair)
    chain_src = stacked(pair_src)
    chips = count // 2
    chip = lax.axis_index("section") // 2
    chain = [(2 * y + 1, 2 * y + 3) for y in range(chips - 1)]
    chain += [(2 * y, 2 * y - 2) for y in range(1, chips)]
    own_map = jnp.stack([real_part, imag_part])
    upstream_map, upstream_src = lax.ppermute((own_map, chain_src), "section", chain)
    has_upstream = jnp.where(odd, chip >= 1, chip <= chips - 2)
    joint_real, joint_imag = matrix_product(own_map, upstream_map)
    joint_real = jnp.where(has_upstream, joint_real, real_part).astype(jnp.bfloat16)
    joint_imag = jnp.where(has_upstream, joint_imag, imag_part).astype(jnp.bfloat16)
    joint_src = (stacked(complex_product(own_map, joined(upstream_src), False))
                 + chain_src).astype(jnp.bfloat16)
    joint_map = jnp.concatenate(
        [
            jnp.concatenate([joint_real, -joint_imag], axis=1),
            jnp.concatenate([joint_imag, joint_real], axis=1),
        ],
        axis=0,
    )
    stride = [(2 * y + 1, 2 * y + 5) for y in range(chips - 2)]
    stride += [(2 * y, 2 * y - 4) for y in range(2, chips)]
    state = joint_src
    for _ in range((chips - 1) // 2):
        arrived = lax.ppermute(state, "section", stride)
        state = (jnp.dot(joint_map, arrived, preferred_element_type=jnp.float32)
                 + joint_src).astype(jnp.bfloat16)
    state = joined(state)
    hand_over = [(s, s + 1) for s in range(1, count - 1, 2)]
    hand_over += [(s, s - 1) for s in range(2, count, 2)]
    neighbour = lax.ppermute(state, "section", hand_over)
    other = lax.cond(
        odd,
        lambda: (complex_product(blocks, neighbour, True) + backward_src).astype(jnp.bfloat16),
        lambda: (complex_product(blocks, neighbour, False) + forward_src).astype(jnp.bfloat16),
    )
    return state, other


SHIFT_ROUNDS = (((1, (0,)), (2, (0,))), ((3, (0, 1)), (4, (1, 2))))


def shifted_copies(sent, direction):
    copies = {0: sent}
    for rounds in SHIFT_ROUNDS:
        arrived = {}
        for step, held in rounds:
            payload = jnp.stack([copies[k] for k in held])
            moved = passed_along(payload, "energy", direction * step)
            for j, k in enumerate(held):
                arrived[k + step] = moved[j]
        copies.update(arrived)
    return copies


def on_device(
    propagator, forward_source, backward_source, left_orbital, right_orbital, phonon_shift, coupling
):
    orbitals = propagator.shape[3]
    modes = forward_source.shape[3] // 2
    own, other = sweeps(propagator[0, 0], forward_source[0, 0], backward_source[0, 0])
    odd = lax.axis_index("section") % 2 == 1
    section_base = lax.axis_index("section") * orbitals
    left_local = left_orbital - section_base
    right_local = right_orbital - section_base
    own_rows = picked_rows(own, jnp.where(odd, left_local, right_local))
    other_rows = picked_rows(other, jnp.where(odd, right_local, left_local))
    real_part = jnp.sum(own_rows * other_rows, axis=0)
    swapped_imag = jnp.sum(own_rows[modes:] * other_rows[:modes], axis=0) - jnp.sum(
        own_rows[:modes] * other_rows[modes:], axis=0
    )
    imag_part = jnp.where(odd, swapped_imag, -swapped_imag)
    lesser_part = jnp.stack([real_part, imag_part]) * modes ** (-0.5)

    sent = lesser_part.astype(jnp.bfloat16)
    moved = {0: lesser_part}
    for direction in (1, -1):
        for k, copy in shifted_copies(sent, direction).items():
            if k != 0:
                moved[direction * k] = copy.astype(jnp.float32)
    self_energy = jnp.zeros_like(lesser_part)
    for offset in range(-MAX_SHIFT, MAX_SHIFT + 1):
        weight = jnp.sum(jnp.where((phonon_shift == offset)[:, None], coupling, 0.0), axis=0)
        self_energy = self_energy + weight[None, :] * moved[offset]
    return self_energy[:, None, :]


def solution(mesh):
    placed = (
        P("energy", "section", None, None, None),
        P("energy", "section", None, None),
        P("energy", "section", None, None),
        P("section"),
        P("section"),
        P(),
        P(None, "section"),
    )
    return jax.shard_map(
        on_device,
        mesh=mesh,
        in_specs=placed,
        out_specs=P(None, "energy", "section"),
        check_vma=False,
    )
```

```python
import jax
import jax.numpy as jnp
from jax import lax
from jax.sharding import PartitionSpec as P

MAX_SHIFT = 6


def passed_along(value, axis, steps):
    count = lax.axis_size(axis)
    leading, last = (max(0, -steps), min(count, count - steps))
    return lax.ppermute(value, axis, [(source, source + steps) for source in range(leading, last)])


def complex_product(matrix, columns, adjoint):
    half = columns.shape[1] // 2
    if adjoint:
        product = jnp.einsum("cji,jn->cin", matrix, columns, preferred_element_type=jnp.float32)
        real_part = product[0, :, :half] + product[1, :, half:]
        imag_part = product[0, :, half:] - product[1, :, :half]
    else:
        product = jnp.einsum("cij,jn->cin", matrix, columns, preferred_element_type=jnp.float32)
        real_part = product[0, :, :half] - product[1, :, half:]
        imag_part = product[0, :, half:] + product[1, :, :half]
    return jnp.concatenate([real_part, imag_part], axis=1)


def matrix_product(left, right):
    product = jnp.einsum("cij,djk->cdik", left, right, preferred_element_type=jnp.float32)
    real_part = product[0, 0] - product[1, 1]
    imag_part = product[0, 1] + product[1, 0]
    return real_part, imag_part


def adjoint_product(left, right):
    product = jnp.einsum("ckj,dji->cdik", left, right, preferred_element_type=jnp.float32)
    real_part = product[0, 0] - product[1, 1]
    imag_part = -(product[0, 1] + product[1, 0])
    return real_part, imag_part


def stacked(columns):
    half = columns.shape[1] // 2
    return jnp.concatenate([columns[:, :half], columns[:, half:]], axis=0)


def joined(rows):
    half = rows.shape[0] // 2
    return jnp.concatenate([rows[:half], rows[half:]], axis=1)


def picked_rows(table, index):
    rows = table.shape[0]
    selector = (lax.broadcasted_iota(jnp.int32, (rows, index.shape[0]), 0) == index[None, :])
    return jnp.einsum(
        "ar,ap->rp", table, selector.astype(table.dtype), preferred_element_type=jnp.float32
    )


def sweeps(blocks, forward_src, backward_src):
    count = lax.axis_size("section")
    odd = lax.axis_index("section") % 2 == 1
    swap = [(2 * y + side, 2 * y + 1 - side) for y in range(count // 2) for side in (0, 1)]
    width = blocks.shape[1]
    packed = jnp.concatenate(
        [blocks[0], blocks[1], jnp.where(odd, backward_src, forward_src)], axis=1
    )
    arrived = lax.ppermute(packed, "section", swap)
    other_blocks = jnp.stack([arrived[:, :width], arrived[:, width:2 * width]])
    other_src = arrived[:, 2 * width:]

    def forward_pair():
        real_part, imag_part = matrix_product(blocks, other_blocks)
        source = complex_product(blocks, other_src, False) + forward_src
        return real_part.astype(jnp.bfloat16), imag_part.astype(jnp.bfloat16), source.astype(
            jnp.bfloat16
        )

    def backward_pair():
        real_part, imag_part = adjoint_product(other_blocks, blocks)
        source = complex_product(blocks, other_src, True) + backward_src
        return real_part.astype(jnp.bfloat16), imag_part.astype(jnp.bfloat16), source.astype(
            jnp.bfloat16
        )

    real_part, imag_part, pair_src = lax.cond(odd, forward_pair, backward_pair)
    chain_src = stacked(pair_src)
    chips = count // 2
    chip = lax.axis_index("section") // 2
    chain = [(2 * y + 1, 2 * y + 3) for y in range(chips - 1)]
    chain += [(2 * y, 2 * y - 2) for y in range(1, chips)]
    own_map = jnp.stack([real_part, imag_part])
    upstream_map, upstream_src = lax.ppermute((own_map, chain_src), "section", chain)
    has_upstream = jnp.where(odd, chip >= 1, chip <= chips - 2)
    joint_real, joint_imag = matrix_product(own_map, upstream_map)
    joint_real = jnp.where(has_upstream, joint_real, real_part).astype(jnp.bfloat16)
    joint_imag = jnp.where(has_upstream, joint_imag, imag_part).astype(jnp.bfloat16)
    joint_src = (stacked(complex_product(own_map, joined(upstream_src), False))
                 + chain_src).astype(jnp.bfloat16)
    joint_map = jnp.concatenate(
        [
            jnp.concatenate([joint_real, -joint_imag], axis=1),
            jnp.concatenate([joint_imag, joint_real], axis=1),
        ],
        axis=0,
    )
    stride = [(2 * y + 1, 2 * y + 5) for y in range(chips - 2)]
    stride += [(2 * y, 2 * y - 4) for y in range(2, chips)]
    state = joint_src
    for _ in range((chips - 1) // 2):
        arrived = lax.ppermute(state, "section", stride)
        state = (jnp.dot(joint_map, arrived, preferred_element_type=jnp.float32)
                 + joint_src).astype(jnp.bfloat16)
    state = joined(state)
    hand_over = [(s, s + 1) for s in range(1, count - 1, 2)]
    hand_over += [(s, s - 1) for s in range(2, count, 2)]
    neighbour = lax.ppermute(state, "section", hand_over)
    other = jnp.where(
        odd,
        (complex_product(blocks, neighbour, True) + backward_src).astype(jnp.bfloat16),
        (complex_product(blocks, neighbour, False) + forward_src).astype(jnp.bfloat16),
    )
    return state, other


SHIFT_ROUNDS = (((1, (0,)), (2, (0,))), ((3, (0, 1)), (4, (1, 2))))


def shifted_copies(sent, direction):
    copies = {0: sent}
    for rounds in SHIFT_ROUNDS:
        arrived = {}
        for step, held in rounds:
            payload = jnp.stack([copies[k] for k in held])
            moved = passed_along(payload, "energy", direction * step)
            for j, k in enumerate(held):
                arrived[k + step] = moved[j]
        copies.update(arrived)
    return copies


def on_device(
    propagator, forward_source, backward_source, left_orbital, right_orbital, phonon_shift, coupling
):
    orbitals = propagator.shape[3]
    modes = forward_source.shape[3] // 2
    own, other = sweeps(propagator[0, 0], forward_source[0, 0], backward_source[0, 0])
    odd = lax.axis_index("section") % 2 == 1
    section_base = lax.axis_index("section") * orbitals
    left_local = left_orbital - section_base
    right_local = right_orbital - section_base
    own_rows = picked_rows(own, jnp.where(odd, left_local, right_local))
    other_rows = picked_rows(other, jnp.where(odd, right_local, left_local))
    real_part = jnp.sum(own_rows * other_rows, axis=0)
    swapped_imag = jnp.sum(own_rows[modes:] * other_rows[:modes], axis=0) - jnp.sum(
        own_rows[:modes] * other_rows[modes:], axis=0
    )
    imag_part = jnp.where(odd, swapped_imag, -swapped_imag)
    lesser_part = jnp.stack([real_part, imag_part]) * modes ** (-0.5)

    sent = lesser_part.astype(jnp.bfloat16)
    moved = {0: lesser_part}
    for direction in (1, -1):
        for k, copy in shifted_copies(sent, direction).items():
            if k != 0:
                moved[direction * k] = copy.astype(jnp.float32)
    self_energy = jnp.zeros_like(lesser_part)
    for offset in range(-MAX_SHIFT, MAX_SHIFT + 1):
        weight = jnp.sum(jnp.where((phonon_shift == offset)[:, None], coupling, 0.0), axis=0)
        self_energy = self_energy + weight[None, :] * moved[offset]
    return self_energy[:, None, :]


def solution(mesh):
    placed = (
        P("energy", "section", None, None, None),
        P("energy", "section", None, None),
        P("energy", "section", None, None),
        P("section"),
        P("section"),
        P(),
        P(None, "section"),
    )
    return jax.shard_map(
        on_device,
        mesh=mesh,
        in_specs=placed,
        out_specs=P(None, "energy", "section"),
        check_vma=False,
    )
```

```python
import jax
import jax.numpy as jnp
from jax import lax
from jax.sharding import PartitionSpec as P

MAX_SHIFT = 6


def passed_along(value, axis, steps):
    count = lax.axis_size(axis)
    leading, last = (max(0, -steps), min(count, count - steps))
    return lax.ppermute(value, axis, [(source, source + steps) for source in range(leading, last)])


def complex_product(matrix, columns, adjoint):
    half = columns.shape[1] // 2
    if adjoint:
        product = jnp.einsum("cji,jn->cin", matrix, columns, preferred_element_type=jnp.float32)
        real_part = product[0, :, :half] + product[1, :, half:]
        imag_part = product[0, :, half:] - product[1, :, :half]
    else:
        product = jnp.einsum("cij,jn->cin", matrix, columns, preferred_element_type=jnp.float32)
        real_part = product[0, :, :half] - product[1, :, half:]
        imag_part = product[0, :, half:] + product[1, :, :half]
    return jnp.concatenate([real_part, imag_part], axis=1)


def matrix_product(left, right):
    product = jnp.einsum("cij,djk->cdik", left, right, preferred_element_type=jnp.float32)
    real_part = product[0, 0] - product[1, 1]
    imag_part = product[0, 1] + product[1, 0]
    return real_part, imag_part


def adjoint_product(left, right):
    product = jnp.einsum("ckj,dji->cdik", left, right, preferred_element_type=jnp.float32)
    real_part = product[0, 0] - product[1, 1]
    imag_part = -(product[0, 1] + product[1, 0])
    return real_part, imag_part


def stacked(columns):
    half = columns.shape[1] // 2
    return jnp.concatenate([columns[:, :half], columns[:, half:]], axis=0)


def joined(rows):
    half = rows.shape[0] // 2
    return jnp.concatenate([rows[:half], rows[half:]], axis=1)


def picked_rows(table, index):
    rows = table.shape[0]
    selector = (lax.broadcasted_iota(jnp.int32, (rows, index.shape[0]), 0) == index[None, :])
    return jnp.einsum(
        "ar,ap->rp", table, selector.astype(table.dtype), preferred_element_type=jnp.float32
    )


def sweeps(blocks, forward_src, backward_src):
    count = lax.axis_size("section")
    odd = lax.axis_index("section") % 2 == 1
    swap = [(2 * y + side, 2 * y + 1 - side) for y in range(count // 2) for side in (0, 1)]
    width = blocks.shape[1]
    packed = jnp.concatenate(
        [blocks[0], blocks[1], jnp.where(odd, backward_src, forward_src)], axis=1
    )
    arrived = lax.ppermute(packed, "section", swap)
    other_blocks = jnp.stack([arrived[:, :width], arrived[:, width:2 * width]])
    other_src = arrived[:, 2 * width:]

    def forward_pair():
        real_part, imag_part = matrix_product(blocks, other_blocks)
        source = complex_product(blocks, other_src, False) + forward_src
        return real_part.astype(jnp.bfloat16), imag_part.astype(jnp.bfloat16), source.astype(
            jnp.bfloat16
        )

    def backward_pair():
        real_part, imag_part = adjoint_product(other_blocks, blocks)
        source = complex_product(blocks, other_src, True) + backward_src
        return real_part.astype(jnp.bfloat16), imag_part.astype(jnp.bfloat16), source.astype(
            jnp.bfloat16
        )

    real_part, imag_part, pair_src = lax.cond(odd, forward_pair, backward_pair)
    chain_src = stacked(pair_src)
    chips = count // 2
    chip = lax.axis_index("section") // 2
    chain = [(2 * y + 1, 2 * y + 3) for y in range(chips - 1)]
    chain += [(2 * y, 2 * y - 2) for y in range(1, chips)]
    own_map = jnp.stack([real_part, imag_part])
    upstream = lax.ppermute(
        jnp.concatenate([real_part, imag_part, joined(chain_src)], axis=1), "section", chain
    )
    upstream_map = jnp.stack([upstream[:, :width], upstream[:, width:2 * width]])
    upstream_src = stacked(upstream[:, 2 * width:])
    has_upstream = jnp.where(odd, chip >= 1, chip <= chips - 2)
    joint_real, joint_imag = matrix_product(own_map, upstream_map)
    joint_real = jnp.where(has_upstream, joint_real, real_part).astype(jnp.bfloat16)
    joint_imag = jnp.where(has_upstream, joint_imag, imag_part).astype(jnp.bfloat16)
    joint_src = (stacked(complex_product(own_map, joined(upstream_src), False))
                 + chain_src).astype(jnp.bfloat16)
    joint_map = jnp.concatenate(
        [
            jnp.concatenate([joint_real, -joint_imag], axis=1),
            jnp.concatenate([joint_imag, joint_real], axis=1),
        ],
        axis=0,
    )
    stride = [(2 * y + 1, 2 * y + 5) for y in range(chips - 2)]
    stride += [(2 * y, 2 * y - 4) for y in range(2, chips)]
    state = joint_src
    for _ in range((chips - 1) // 2):
        arrived = lax.ppermute(state, "section", stride)
        state = (jnp.dot(joint_map, arrived, preferred_element_type=jnp.float32)
                 + joint_src).astype(jnp.bfloat16)
    state = joined(state)
    hand_over = [(s, s + 1) for s in range(1, count - 1, 2)]
    hand_over += [(s, s - 1) for s in range(2, count, 2)]
    neighbour = lax.ppermute(state, "section", hand_over)
    other = jnp.where(
        odd,
        (complex_product(blocks, neighbour, True) + backward_src).astype(jnp.bfloat16),
        (complex_product(blocks, neighbour, False) + forward_src).astype(jnp.bfloat16),
    )
    return state, other


SHIFT_ROUNDS = (((1, (0,)), (2, (0,))), ((3, (0, 1)), (4, (1, 2))))


def shifted_copies(sent, direction):
    copies = {0: sent}
    for rounds in SHIFT_ROUNDS:
        arrived = {}
        for step, held in rounds:
            payload = jnp.stack([copies[k] for k in held])
            moved = passed_along(payload, "energy", direction * step)
            for j, k in enumerate(held):
                arrived[k + step] = moved[j]
        copies.update(arrived)
    return copies


def on_device(
    propagator, forward_source, backward_source, left_orbital, right_orbital, phonon_shift, coupling
):
    orbitals = propagator.shape[3]
    modes = forward_source.shape[3] // 2
    own, other = sweeps(propagator[0, 0], forward_source[0, 0], backward_source[0, 0])
    odd = lax.axis_index("section") % 2 == 1
    section_base = lax.axis_index("section") * orbitals
    left_local = left_orbital - section_base
    right_local = right_orbital - section_base
    own_rows = picked_rows(own, jnp.where(odd, left_local, right_local))
    other_rows = picked_rows(other, jnp.where(odd, right_local, left_local))
    real_part = jnp.sum(own_rows * other_rows, axis=0)
    swapped_imag = jnp.sum(own_rows[modes:] * other_rows[:modes], axis=0) - jnp.sum(
        own_rows[:modes] * other_rows[modes:], axis=0
    )
    imag_part = jnp.where(odd, swapped_imag, -swapped_imag)
    lesser_part = jnp.stack([real_part, imag_part]) * modes ** (-0.5)

    sent = lesser_part.astype(jnp.bfloat16)
    moved = {0: lesser_part}
    for direction in (1, -1):
        for k, copy in shifted_copies(sent, direction).items():
            if k != 0:
                moved[direction * k] = copy.astype(jnp.float32)
    self_energy = jnp.zeros_like(lesser_part)
    for offset in range(-MAX_SHIFT, MAX_SHIFT + 1):
        weight = jnp.sum(jnp.where((phonon_shift == offset)[:, None], coupling, 0.0), axis=0)
        self_energy = self_energy + weight[None, :] * moved[offset]
    return self_energy[:, None, :]


def solution(mesh):
    placed = (
        P("energy", "section", None, None, None),
        P("energy", "section", None, None),
        P("energy", "section", None, None),
        P("section"),
        P("section"),
        P(),
        P(None, "section"),
    )
    return jax.shard_map(
        on_device,
        mesh=mesh,
        in_specs=placed,
        out_specs=P(None, "energy", "section"),
        check_vma=False,
    )
```

```python
import jax
import jax.numpy as jnp
from jax import lax
from jax.sharding import PartitionSpec as P

MAX_SHIFT = 6


def passed_along(value, axis, steps):
    count = lax.axis_size(axis)
    leading, last = (max(0, -steps), min(count, count - steps))
    return lax.ppermute(value, axis, [(source, source + steps) for source in range(leading, last)])


def complex_product(matrix, columns, adjoint):
    half = columns.shape[1] // 2
    if adjoint:
        product = jnp.einsum("cji,jn->cin", matrix, columns, preferred_element_type=jnp.float32)
        real_part = product[0, :, :half] + product[1, :, half:]
        imag_part = product[0, :, half:] - product[1, :, :half]
    else:
        product = jnp.einsum("cij,jn->cin", matrix, columns, preferred_element_type=jnp.float32)
        real_part = product[0, :, :half] - product[1, :, half:]
        imag_part = product[0, :, half:] + product[1, :, :half]
    return jnp.concatenate([real_part, imag_part], axis=1)


def matrix_product(left, right):
    product = jnp.einsum("cij,djk->cdik", left, right, preferred_element_type=jnp.float32)
    real_part = product[0, 0] - product[1, 1]
    imag_part = product[0, 1] + product[1, 0]
    return real_part, imag_part


def adjoint_product(left, right):
    product = jnp.einsum("ckj,dji->cdik", left, right, preferred_element_type=jnp.float32)
    real_part = product[0, 0] - product[1, 1]
    imag_part = -(product[0, 1] + product[1, 0])
    return real_part, imag_part


def stacked(columns):
    half = columns.shape[1] // 2
    return jnp.concatenate([columns[:, :half], columns[:, half:]], axis=0)


def joined(rows):
    half = rows.shape[0] // 2
    return jnp.concatenate([rows[:half], rows[half:]], axis=1)


def picked_rows(table, index):
    rows = table.shape[0]
    selector = (lax.broadcasted_iota(jnp.int32, (rows, index.shape[0]), 0) == index[None, :])
    return jnp.einsum(
        "ar,ap->rp", table, selector.astype(table.dtype), preferred_element_type=jnp.float32
    )


def sweeps(blocks, forward_src, backward_src):
    count = lax.axis_size("section")
    odd = lax.axis_index("section") % 2 == 1
    swap = [(2 * y + side, 2 * y + 1 - side) for y in range(count // 2) for side in (0, 1)]
    width = blocks.shape[1]
    modes2 = forward_src.shape[1]
    packed = jnp.concatenate([blocks[0], blocks[1], forward_src, backward_src], axis=1)
    arrived = lax.ppermute(packed, "section", swap)
    other_blocks = jnp.stack([arrived[:, :width], arrived[:, width:2 * width]])
    other_forward = arrived[:, 2 * width:2 * width + modes2]
    other_backward = arrived[:, 2 * width + modes2:]

    def forward_pair():
        real_part, imag_part = matrix_product(blocks, other_blocks)
        source = complex_product(blocks, other_forward, False) + forward_src
        return real_part.astype(jnp.bfloat16), imag_part.astype(jnp.bfloat16), source.astype(
            jnp.bfloat16
        )

    def backward_pair():
        real_part, imag_part = adjoint_product(other_blocks, blocks)
        source = complex_product(blocks, other_backward, True) + backward_src
        return real_part.astype(jnp.bfloat16), imag_part.astype(jnp.bfloat16), source.astype(
            jnp.bfloat16
        )

    real_part, imag_part, pair_src = lax.cond(odd, forward_pair, backward_pair)
    chain_src = stacked(pair_src)
    chips = count // 2
    chip = lax.axis_index("section") // 2
    chain = [(2 * y + 1, 2 * y + 3) for y in range(chips - 1)]
    chain += [(2 * y, 2 * y - 2) for y in range(1, chips)]
    own_map = jnp.stack([real_part, imag_part])
    upstream_map, upstream_src = lax.ppermute((own_map, chain_src), "section", chain)
    has_upstream = jnp.where(odd, chip >= 1, chip <= chips - 2)
    joint_real, joint_imag = matrix_product(own_map, upstream_map)
    joint_real = jnp.where(has_upstream, joint_real, real_part).astype(jnp.bfloat16)
    joint_imag = jnp.where(has_upstream, joint_imag, imag_part).astype(jnp.bfloat16)
    joint_src = (stacked(complex_product(own_map, joined(upstream_src), False))
                 + chain_src).astype(jnp.bfloat16)
    joint_map = jnp.concatenate(
        [
            jnp.concatenate([joint_real, -joint_imag], axis=1),
            jnp.concatenate([joint_imag, joint_real], axis=1),
        ],
        axis=0,
    )
    stride = [(2 * y + 1, 2 * y + 5) for y in range(chips - 2)]
    stride += [(2 * y, 2 * y - 4) for y in range(2, chips)]
    state = joint_src
    for _ in range((chips - 1) // 2):
        arrived = lax.ppermute(state, "section", stride)
        state = (jnp.dot(joint_map, arrived, preferred_element_type=jnp.float32)
                 + joint_src).astype(jnp.bfloat16)
    state = joined(state)
    hand_over = [(s, s + 1) for s in range(1, count - 1, 2)]
    hand_over += [(s, s - 1) for s in range(2, count, 2)]
    neighbour = lax.ppermute(state, "section", hand_over)
    other = jnp.where(
        odd,
        (complex_product(blocks, neighbour, True) + backward_src).astype(jnp.bfloat16),
        (complex_product(blocks, neighbour, False) + forward_src).astype(jnp.bfloat16),
    )
    return state, other


SHIFT_ROUNDS = (((1, (0,)), (2, (0,))), ((3, (0, 1)), (4, (1, 2))))


def shifted_copies(sent, direction):
    copies = {0: sent}
    for rounds in SHIFT_ROUNDS:
        arrived = {}
        for step, held in rounds:
            payload = jnp.stack([copies[k] for k in held])
            moved = passed_along(payload, "energy", direction * step)
            for j, k in enumerate(held):
                arrived[k + step] = moved[j]
        copies.update(arrived)
    return copies


def on_device(
    propagator, forward_source, backward_source, left_orbital, right_orbital, phonon_shift, coupling
):
    orbitals = propagator.shape[3]
    modes = forward_source.shape[3] // 2
    own, other = sweeps(propagator[0, 0], forward_source[0, 0], backward_source[0, 0])
    odd = lax.axis_index("section") % 2 == 1
    section_base = lax.axis_index("section") * orbitals
    left_local = left_orbital - section_base
    right_local = right_orbital - section_base
    own_rows = picked_rows(own, jnp.where(odd, left_local, right_local))
    other_rows = picked_rows(other, jnp.where(odd, right_local, left_local))
    real_part = jnp.sum(own_rows * other_rows, axis=0)
    swapped_imag = jnp.sum(own_rows[modes:] * other_rows[:modes], axis=0) - jnp.sum(
        own_rows[:modes] * other_rows[modes:], axis=0
    )
    imag_part = jnp.where(odd, swapped_imag, -swapped_imag)
    lesser_part = jnp.stack([real_part, imag_part]) * modes ** (-0.5)

    sent = lesser_part.astype(jnp.bfloat16)
    moved = {0: lesser_part}
    for direction in (1, -1):
        for k, copy in shifted_copies(sent, direction).items():
            if k != 0:
                moved[direction * k] = copy.astype(jnp.float32)
    self_energy = jnp.zeros_like(lesser_part)
    for offset in range(-MAX_SHIFT, MAX_SHIFT + 1):
        weight = jnp.sum(jnp.where((phonon_shift == offset)[:, None], coupling, 0.0), axis=0)
        self_energy = self_energy + weight[None, :] * moved[offset]
    return self_energy[:, None, :]


def solution(mesh):
    placed = (
        P("energy", "section", None, None, None),
        P("energy", "section", None, None),
        P("energy", "section", None, None),
        P("section"),
        P("section"),
        P(),
        P(None, "section"),
    )
    return jax.shard_map(
        on_device,
        mesh=mesh,
        in_specs=placed,
        out_specs=P(None, "energy", "section"),
        check_vma=False,
    )
```
